32 devices in a mesh: tract: 2 (over x), skyx: 4 (over y, core), skyy: 4 (over z).
Axes of the slice: x: 2, y: 2, z: 4, core: 2. Of those that a mesh axis runs over, the one named last changes fastest.
Arguments:
- images: bfloat16 [8, 8, 136, 4480], P(('tract', 'skyy'), 'skyx'), parts along dimension 0, may hold values from -6 to 6
- masks: int32 [8, 8, 136, 4480], P(('tract', 'skyy'), 'skyx'), parts along dimension 0, may hold values 0 or 1
- row_kernels: bfloat16 [8, 8, 128, 136], P(('tract', 'skyy'), 'skyx'), parts along dimension 0, may hold values from -1 to 2
- col_kernel: bfloat16 [66, 384, 128], P('tract'), parts along dimension 0, may hold values from -1 to 2
- inv_var: float32 [8, 8], P(('tract', 'skyy')), parts along dimension 0, may hold values from 0.5 to 4
- dest_col: int32 [8, 128, 1], P(('tract', 'skyy'), 'skyx'), parts along dimension 0, may hold values from 0 to 3; in each aligned block of 32 rows (0 to 31, 32 to 63, ..., all dimensions but the last counted through in order) at most 12 rows name the same one
- dest_row: int32 [8, 128], P(('tract', 'skyy'), 'skyx'), parts along dimension 0, may hold values from 0 to 31
Outputs:
- coadd: float32 [1024, 15872], P(('tract', 'skyy'), 'skyx'), parts along dimension 0
The draws below stay inside these ranges and needn't reach their ends.
There are 2 independent parts, one for each index of `tract`. The reference program is written for one: setup_inputs(seed, part) draws one part's arguments, and reference() takes and returns one part's arrays. A program takes and returns all parts, laid end to end along the dimension named above; each array names one. Nothing has to cross between parts.
Inputs may be any that keep to these rules, and one draw needn't show every extreme that they name: `dest_col`: the 32 row blocks of any one device name one patch column at most 12 times, and some device names one exactly 12 times.
All inputs are finite; a program needn't handle non-finite values. No bound on the sum of `masks` on one device may be relied on, other than what follows from the above.
Results may differ from the reference program's by a relative error of at most 0.0057.
Values may be sent and summed in bfloat16 or wider, within the bound.
No kernel may reach another device: no remote copies, remote signals or barrier semaphores. Data moves between devices by JAX's collectives and lax.ppermute only.
A program may use at most 128 MiB of HBM per device.

```python
import math
import jax
import jax.numpy as jnp
import numpy as np
from jax import lax

PW = 3968
OVX = 128
OVY = 64
PR = 128
PH = 128
RB = 8
EXP_DEV = 2
HIN = 136
CW = 4224
WIN = 4480
TILES = 33
KW = 384
CR = 256
NPOS = 32
SLOTS = 32
CAP = 12
N_SKYX = 4
N_SKYY = 4


def draw_row_kernels(key, part):
    shape = (N_SKYY, N_SKYX * EXP_DEV, PH, HIN)
    out_index = lax.broadcasted_iota(jnp.int32, shape, 2)
    in_index = lax.broadcasted_iota(jnp.int32, shape, 3)
    peaked = (in_index == out_index + 4).astype(jnp.float32)
    noisy = jax.random.normal(key, shape, jnp.float32) * 0.2
    return (peaked + noisy * HIN ** (-0.5)).astype(jnp.bfloat16)


def draw_col_kernel(key, part):
    shape = (TILES, KW, OVX)
    in_index = lax.broadcasted_iota(jnp.int32, shape, 1)
    out_index = lax.broadcasted_iota(jnp.int32, shape, 2)
    peaked = (in_index == out_index + OVX).astype(jnp.float32)
    noisy = jax.random.normal(key, shape, jnp.float32) * 0.2
    return (peaked + noisy * KW ** (-0.5)).astype(jnp.bfloat16)


def plant(drawn, own_key, least, high):
    place = [jax.random.randint(jax.random.fold_in(own_key, axis), (), 0, length) for axis, length in enumerate(drawn.shape)]
    longest = drawn.shape.index(max(drawn.shape))
    beside = place[:longest] + [(place[longest] + 1) % drawn.shape[longest]] + place[longest + 1:]
    return drawn.at[tuple(place)].set(least).at[tuple(beside)].set(high)


def levels(stream_key, dims, pieces, smallest, largest):
    level = 1.0
    for axis_at, blocks in pieces:
        draws = jax.random.uniform(jax.random.fold_in(jax.random.fold_in(stream_key, 6), axis_at), (blocks,), jnp.float32, smallest / len(pieces), largest / len(pieces))
        level = level * jnp.repeat(jnp.exp(draws), dims[axis_at] // blocks).reshape((-1,) + (1,) * (len(dims) - 1 - axis_at))
    return level


def deal_out(own_key, own, number, rows, amount, top, bound, slope):
    ranking = jax.random.permutation(own_key, amount)
    crowded, ordinary = shares(amount, rows * top, bound, slope, True), shares(amount, rows * top, bound, slope, False)
    places = jnp.arange(amount)

    def named(sizes, offset_by):
        used = int((sizes > 0).sum())
        fixed = max(1, used // 4)
        passed = fixed + (places - fixed + offset_by * (used - fixed)) % max(1, amount - fixed)
        return jnp.zeros((amount,), jnp.int32).at[ranking[jnp.where(places < fixed, places, passed)]].set(jnp.asarray(sizes, jnp.int32))

    sizes = jnp.where(number % 4 == 0, named(crowded, number // 4), named(ordinary, number - number // 4 - 1))
    mixed = jax.random.permutation(jax.random.fold_in(own, 3), amount)
    donor, receiver = mixed[0:amount // 2 * 2:2], mixed[1:amount // 2 * 2:2]
    room = jnp.minimum(sizes[donor] - 1, bound - sizes[receiver]) // 2
    room = jnp.where((donor == ranking[0]) | (receiver == ranking[0]) | (sizes[receiver] == 0), 0, jnp.maximum(room, 0))
    passed = jax.random.randint(jax.random.fold_in(own, 4), (amount // 2,), 0, 1 << 20) % (room + 1)
    sizes = sizes.at[donor].add(-passed).at[receiver].add(passed)
    labels = jnp.searchsorted(jnp.cumsum(sizes), jnp.arange(rows * top), side="right").astype(jnp.int32)
    table = labels.reshape(top, rows).T
    table = table[jax.random.permutation(jax.random.fold_in(own, 1), rows)]
    offset_by = jax.random.randint(jax.random.fold_in(own, 2), (rows, 1), 0, top)
    return jnp.take_along_axis(table, (jnp.arange(top)[None, :] + offset_by) % top, axis=1)


def shares(amount, total, most, slope, full):
    weights = [(1 << 20) // math.isqrt(rank ** slope) + 1 for rank in range(1, amount + 1)]
    largest = most if full else min(most, max(-(-total // amount), total * weights[0] // sum(weights)))
    least = 1 if total - largest >= amount - 1 else 0
    given, surplus = [largest] + [least] * (amount - 1), total - largest - least * (amount - 1)
    while surplus > 0:
        candidates = [i for i in range(1, amount) if given[i] < largest] or [i for i in range(1, amount) if given[i] < most]
        whole, remaining = sum([weights[i] for i in candidates]), surplus
        for i in candidates:
            more = min(most - given[i], max(1, remaining * weights[i] // whole), surplus)
            given[i] = given[i] + more
            surplus = surplus - more
    return np.array(given)


def gaussian(stream_key, dims, scale, limit, shards=(), dtype=jnp.bfloat16):
    values = scale * jax.random.normal(stream_key, dims, jnp.float32)
    if shards:
        values = values * levels(stream_key, dims, shards, -0.22, 0.18)
    return jnp.clip(values, -limit, limit).astype(dtype)


def setup_inputs(seed: int = 0, part: int = 0) -> dict:
    splits = jax.random.split(jax.random.key(seed), 8)
    own_keys = jax.random.split(jax.random.fold_in(splits[7], part), 8)
    images = gaussian(own_keys[0], (N_SKYY, N_SKYX * EXP_DEV, HIN, WIN), 1.0, 6.0, ((0, 4), (1, 4)))
    masks = plant((jax.random.randint(own_keys[1], (N_SKYY, N_SKYX * EXP_DEV, HIN, WIN), 0, 8) < 1).astype(jnp.int32), jax.random.fold_in(own_keys[1], 1), 0, 1)
    row_kernels = draw_row_kernels(jax.random.fold_in(jax.random.fold_in(splits[7], part), 71), part)
    col_kernel = draw_col_kernel(jax.random.fold_in(jax.random.fold_in(splits[7], part), 71), part)
    inv_var = jnp.clip(jnp.exp(math.log(4.0) - 2.0794415 * jax.random.uniform(own_keys[4], (N_SKYY, N_SKYX * EXP_DEV), jnp.float32) ** levels(own_keys[4], (N_SKYY, N_SKYX * EXP_DEV), ((0, 4),), -0.2, 0.2)), 0.5, 4.0)
    dest_col_keys = jax.random.split(jax.random.fold_in(own_keys[5], 1), N_SKYY * (N_SKYX * SLOTS) // SLOTS)
    dest_col_turns = jax.random.permutation(jax.random.fold_in(own_keys[5], 3), N_SKYY * (N_SKYX * SLOTS) // SLOTS)
    dest_col = jax.vmap(lambda own, number: deal_out(jax.random.fold_in(own_keys[5], 2), own, number, SLOTS, N_SKYX, 1, CAP, 2))(dest_col_keys, dest_col_turns).reshape((N_SKYY, N_SKYX * SLOTS, 1))
    dest_row = plant(jax.random.randint(own_keys[6], (N_SKYY, N_SKYX * SLOTS), 0, NPOS), jax.random.fold_in(own_keys[6], 1), 0, NPOS - 1).astype(jnp.int32)
    return {"images": images, "masks": masks, "row_kernels": row_kernels, "col_kernel": col_kernel, "inv_var": inv_var, "dest_col": dest_col, "dest_row": dest_row}


def resample_columns(row_warped, col_kernel):
    tile_count = col_kernel.shape[0]
    tile_width = col_kernel.shape[2]
    full_span = tile_count * tile_width
    leading = row_warped.shape[:-1]
    summed = jnp.zeros(leading + (tile_count, tile_width), jnp.float32)
    for shift_tile in range(3):
        window = row_warped[..., shift_tile * tile_width:shift_tile * tile_width + full_span]
        window = window.reshape(leading + (tile_count, tile_width)).astype(jnp.float32)
        kernel_part = col_kernel[:, shift_tile * tile_width:(shift_tile + 1) * tile_width, :].astype(jnp.float32)
        summed = summed + jnp.einsum('...tk,tkj->...tj', window, kernel_part)
    return summed.reshape(leading + (full_span,))


def warp_exposure(packed, col_kernel):
    exposure, mask_plane, row_kernel, weight = packed
    good_pix = (mask_plane == 0).astype(jnp.bfloat16)
    planes = jnp.stack([exposure * good_pix, good_pix], axis=1)
    row_warped = jnp.einsum('qh,hpw->qpw', row_kernel.astype(jnp.float32), planes.astype(jnp.float32)).astype(jnp.bfloat16)
    warped = resample_columns(row_warped, col_kernel)
    return (weight * warped).astype(jnp.bfloat16)


def fold_columns(canvas):
    inner_part = canvas[..., OVX:OVX + PW]
    right_part = canvas[..., OVX + PW:]
    left_part = canvas[..., :OVX]
    zero_col = jnp.zeros_like(right_part[:1])
    from_left = jnp.concatenate([zero_col, right_part[:-1]], axis=0)
    from_right = jnp.concatenate([left_part[1:], zero_col], axis=0)
    inner_part = inner_part.at[..., :OVX].add(from_left)
    inner_part = inner_part.at[..., PW - OVX:].add(from_right)
    return inner_part


def fold_rows(folded):
    inner_part = folded[:, :, OVY:OVY + PR]
    lower_part = folded[:, :, OVY + PR:]
    upper_part = folded[:, :, :OVY]
    zero_row = jnp.zeros_like(lower_part[:1])
    from_above = jnp.concatenate([zero_row, lower_part[:-1]], axis=0)
    from_below = jnp.concatenate([upper_part[1:], zero_row], axis=0)
    inner_part = inner_part.at[:, :, :OVY].add(from_above)
    inner_part = inner_part.at[:, :, PR - OVY:].add(from_below)
    return inner_part


def reference(images, masks, row_kernels, col_kernel, inv_var, dest_col, dest_row):
    rows_sky = images.shape[0]
    total_exp = images.shape[0] * images.shape[1]
    flat_args = (images.reshape((total_exp,) + images.shape[2:]),
                 masks.reshape((total_exp,) + masks.shape[2:]),
                 row_kernels.reshape((total_exp,) + row_kernels.shape[2:]),
                 inv_var.reshape(total_exp))
    warped = lax.map(lambda packed: warp_exposure(packed, col_kernel), flat_args)
    blocks = warped.reshape(rows_sky, N_SKYX * SLOTS, RB, 2, CW)
    targets = (dest_col[:, :, 0] * NPOS + dest_row).astype(jnp.int32)

    def one_row(packed):
        row_blocks, row_targets = packed
        canvas = jax.ops.segment_sum(row_blocks.astype(jnp.float32), row_targets, num_segments=N_SKYX * NPOS)
        canvas = canvas.reshape(N_SKYX, CR, 2, CW)
        return fold_columns(canvas)

    folded = lax.map(one_row, (blocks, targets))
    interior = fold_rows(folded)
    coadd_vals = interior[:, :, :, 0, :] / jnp.maximum(interior[:, :, :, 1, :], 1.0)
    return coadd_vals.transpose(0, 2, 1, 3).reshape(rows_sky * PR, N_SKYX * PW)
```

```python
import jax
import jax.numpy as jnp
from jax import lax
from jax.experimental import pallas as pl
from jax.experimental.pallas import tpu as pltpu
from jax.sharding import PartitionSpec as P

OVY = 64
PR = 128
RB = 8
ROW_CHUNK = 640


def shifted(value, axis, steps):
    count = lax.axis_size(axis)
    first, last = (max(0, -steps), min(count, count - steps))
    return lax.ppermute(value, axis, [(source, source + steps) for source in range(first, last)])


def warp_kernel(w_ref, img_ref, mask_ref, rk_ref, ck_ref, out_ref, rw_ref):
    e = pl.program_id(0)
    ph = rk_ref.shape[2]
    win = img_ref.shape[3]
    tiles, kw, tw = ck_ref.shape
    rk = rk_ref[0, 0]
    for c in range(win // ROW_CHUNK):
        cols = pl.ds(c * ROW_CHUNK, ROW_CHUNK)
        good = mask_ref[0, 0, :, cols] == 0
        img = img_ref[0, 0, :, cols]
        p0 = jnp.where(good, img, jnp.zeros_like(img))
        p1 = good.astype(jnp.bfloat16)
        rw_ref[0:ph, cols] = jnp.dot(rk, p0, preferred_element_type=jnp.float32).astype(jnp.bfloat16)
        rw_ref[ph : 2 * ph, cols] = jnp.dot(rk, p1, preferred_element_type=jnp.float32).astype(jnp.bfloat16)
    weight = w_ref[e]
    blocks = ph // RB

    def tile(t, carry):
        off = pl.multiple_of(t * tw, tw)
        x = rw_ref[:, pl.ds(off, kw)]
        r = jnp.dot(x, ck_ref[t], preferred_element_type=jnp.float32) * weight
        out_ref[:, 0, :, pl.ds(off, tw)] = r[0:ph].reshape(blocks, RB, tw).astype(jnp.bfloat16)
        out_ref[:, 1, :, pl.ds(off, tw)] = r[ph : 2 * ph].reshape(blocks, RB, tw).astype(jnp.bfloat16)
        return carry

    lax.fori_loop(0, tiles, tile, 0)


def warp(weights, images, masks, row_kernels, col_kernel):
    _, exposures, hin, win = images.shape
    ph = row_kernels.shape[2]
    tiles, kw, tw = col_kernel.shape
    cw = tiles * tw
    blocks = ph // RB
    return pl.pallas_call(
        warp_kernel,
        grid=(exposures,),
        in_specs=[
            pl.BlockSpec(memory_space=pltpu.SMEM),
            pl.BlockSpec((1, 1, hin, win), lambda e: (0, e, 0, 0)),
            pl.BlockSpec((1, 1, hin, win), lambda e: (0, e, 0, 0)),
            pl.BlockSpec((1, 1, ph, hin), lambda e: (0, e, 0, 0)),
            pl.BlockSpec((tiles, kw, tw), lambda e: (0, 0, 0)),
        ],
        out_specs=pl.BlockSpec((blocks, 2, RB, cw), lambda e: (e, 0, 0, 0)),
        out_shape=jax.ShapeDtypeStruct((exposures * blocks, 2, RB, cw), jnp.bfloat16),
        scratch_shapes=[pltpu.VMEM((2 * ph, win), jnp.bfloat16)],
        compiler_params=pltpu.CompilerParams(vmem_limit_bytes=56 * 1024 * 1024),
    )(weights, images, masks, row_kernels, col_kernel)


def local(images, masks, row_kernels, col_kernel, inv_var, dest_col, dest_row):
    exposures = images.shape[1]
    tile_width = col_kernel.shape[2]
    cw = col_kernel.shape[0] * tile_width
    pw = cw - 2 * tile_width
    first_exp = lax.axis_index("skyx") * exposures
    weights = lax.dynamic_slice_in_dim(inv_var[0], first_exp, exposures)
    blocks = warp(weights, images, masks, row_kernels, col_kernel)

    slot_dest = dest_col[0, :, 0]
    slot_rows = dest_row[0]
    slot_count = slot_dest.shape[0]
    peers = lax.axis_size("skyx")
    capacity = max(2, (3 * slot_count + 2 * peers - 1) // (2 * peers))
    positions = (PR + 2 * OVY) // RB
    earlier = (jnp.arange(slot_count)[None, :] < jnp.arange(slot_count)[:, None]).astype(jnp.int32)
    onehot_dest = (slot_dest[:, None] == jnp.arange(peers)[None, :]).astype(jnp.int32)
    ranks = jnp.sum(jnp.dot(earlier, onehot_dest) * onehot_dest, axis=1)
    chosen = (slot_dest[None, None, :] == jnp.arange(peers)[:, None, None]) & (
        ranks[None, None, :] == jnp.arange(capacity)[None, :, None]
    )
    send_rows = jnp.sum(jnp.where(chosen, slot_rows[None, None, :] + 1, 0), axis=2) - 1
    send_idx = jnp.sum(jnp.where(chosen, jnp.arange(slot_count)[None, None, :] + 1, 0), axis=2) - 1
    send_idx = jnp.where(send_idx < 0, slot_count, send_idx)
    send_buf = jnp.take(blocks, send_idx.reshape(-1), axis=0, mode="fill", fill_value=0)
    send_buf = send_buf.reshape((peers, capacity) + blocks.shape[1:])
    arrived = lax.all_to_all(send_buf, "skyx", split_axis=0, concat_axis=0, tiled=True)
    recv_rows = lax.all_to_all(send_rows, "skyx", split_axis=0, concat_axis=0, tiled=True)
    arrived = arrived.reshape((-1,) + blocks.shape[1:])
    onehot_pos = (recv_rows.reshape(-1)[:, None] == jnp.arange(positions)[None, :]).astype(jnp.bfloat16)
    canvas = jnp.einsum("sn,sprw->nprw", onehot_pos, arrived, preferred_element_type=jnp.float32)

    margin = OVY // RB
    inner = PR // RB
    upper = canvas[:margin].astype(jnp.bfloat16)
    lower = canvas[margin + inner :].astype(jnp.bfloat16)
    from_above = shifted(lower, "skyy", 1).astype(jnp.float32)
    from_below = shifted(upper, "skyy", -1).astype(jnp.float32)
    interior = canvas[margin : margin + inner]
    interior = interior.at[:margin].add(from_above)
    interior = interior.at[inner - margin :].add(from_below)

    left_part = interior[..., :tile_width].astype(jnp.bfloat16)
    right_part = interior[..., tile_width + pw :].astype(jnp.bfloat16)
    from_left = shifted(right_part, "skyx", 1).astype(jnp.float32)
    from_right = shifted(left_part, "skyx", -1).astype(jnp.float32)
    core = interior[..., tile_width : tile_width + pw]
    core = core.at[..., :tile_width].add(from_left)
    core = core.at[..., pw - tile_width :].add(from_right)
    num = core[:, 0].reshape(PR, pw)
    den = core[:, 1].reshape(PR, pw)
    return num / jnp.maximum(den, 1.0)


def solution(mesh):
    in_specs = (
        P(("tract", "skyy"), "skyx", None, None),
        P(("tract", "skyy"), "skyx", None, None),
        P(("tract", "skyy"), "skyx", None, None),
        P("tract", None, None),
        P(("tract", "skyy"), None),
        P(("tract", "skyy"), "skyx", None),
        P(("tract", "skyy"), "skyx"),
    )
    out_specs = P(("tract", "skyy"), "skyx")
    return jax.shard_map(local, mesh=mesh, in_specs=in_specs, out_specs=out_specs, check_vma=False)
```

```python
import jax
import jax.numpy as jnp
from jax import lax
from jax.experimental import pallas as pl
from jax.experimental.pallas import tpu as pltpu
from jax.sharding import PartitionSpec as P

OVY = 64
PR = 128
RB = 8
CHUNKS = 3
ROW_PIECE = 640


def shifted(value, axis, steps):
    count = lax.axis_size(axis)
    first, last = (max(0, -steps), min(count, count - steps))
    return lax.ppermute(value, axis, [(source, source + steps) for source in range(first, last)])


def make_warp_kernel(start, width, exposures):
    def kernel(w_ref, idx_ref, img_hbm, mask_hbm, rk_ref, ck_ref, out_ref, img_buf, mask_buf, rw_buf, blk_buf, sems):
        ph = rk_ref.shape[2]
        tiles, kw, tw = ck_ref.shape
        blocks = ph // RB
        copies = []
        for e in range(exposures):
            ci = pltpu.make_async_copy(img_hbm.at[0, e, :, pl.ds(start, width)], img_buf.at[e], sems.at[0, e])
            cm = pltpu.make_async_copy(mask_hbm.at[0, e, :, pl.ds(start, width)], mask_buf.at[e], sems.at[1, e])
            ci.start()
            cm.start()
            copies.append((ci, cm))
        for e in range(exposures):
            ci, cm = copies[e]
            ci.wait()
            cm.wait()
            rk = rk_ref[0, e]
            piece_start = 0
            while piece_start < width:
                piece = min(ROW_PIECE, width - piece_start)
                cols = pl.ds(piece_start, piece)
                good = mask_buf[e, :, cols] == 0
                img = img_buf[e, :, cols]
                p0 = jnp.where(good, img, jnp.zeros_like(img))
                p1 = good.astype(jnp.bfloat16)
                rw_buf[0:ph, cols] = jnp.dot(rk, p0, preferred_element_type=jnp.float32).astype(jnp.bfloat16)
                rw_buf[ph : 2 * ph, cols] = jnp.dot(rk, p1, preferred_element_type=jnp.float32).astype(jnp.bfloat16)
                piece_start += piece
            weight = w_ref[e]

            def tile(t, carry):
                off = pl.multiple_of(t * tw, tw)
                x = rw_buf[:, pl.ds(off, kw)]
                r = jnp.dot(x, ck_ref[t], preferred_element_type=jnp.float32) * weight
                rows = pl.ds(e * blocks, blocks)
                blk_buf[rows, 0, :, pl.ds(off, tw)] = r[0:ph].reshape(blocks, RB, tw).astype(jnp.bfloat16)
                blk_buf[rows, 1, :, pl.ds(off, tw)] = r[ph : 2 * ph].reshape(blocks, RB, tw).astype(jnp.bfloat16)
                return carry

            lax.fori_loop(0, tiles, tile, 0)

        def gather(slot, carry):
            out_ref[slot] = blk_buf[idx_ref[slot]]
            return carry

        lax.fori_loop(0, out_ref.shape[0], gather, 0)

    return kernel


def warp_chunk(chunk, weights, send_idx, images, masks, row_kernels, col_kernel):
    _, exposures, hin, win = images.shape
    ph = row_kernels.shape[2]
    tiles, kw, tw = col_kernel.shape
    per = tiles // CHUNKS
    width = per * tw
    window = width + kw - tw
    start = chunk * width
    blocks = ph // RB
    slots = send_idx.shape[0]
    return pl.pallas_call(
        make_warp_kernel(start, window, exposures),
        grid=(1,),
        in_specs=[
            pl.BlockSpec(memory_space=pltpu.SMEM),
            pl.BlockSpec(memory_space=pltpu.SMEM),
            pl.BlockSpec(memory_space=pl.ANY),
            pl.BlockSpec(memory_space=pl.ANY),
            pl.BlockSpec(memory_space=pltpu.VMEM),
            pl.BlockSpec((per, kw, tw), lambda i: (chunk, 0, 0)),
        ],
        out_specs=pl.BlockSpec(memory_space=pltpu.VMEM),
        out_shape=jax.ShapeDtypeStruct((slots, 2, RB, width), jnp.bfloat16),
        scratch_shapes=[
            pltpu.VMEM((exposures, hin, window), jnp.bfloat16),
            pltpu.VMEM((exposures, hin, window), jnp.int32),
            pltpu.VMEM((2 * ph, window), jnp.bfloat16),
            pltpu.VMEM((exposures * blocks, 2, RB, width), jnp.bfloat16),
            pltpu.SemaphoreType.DMA((2, exposures)),
        ],
        compiler_params=pltpu.CompilerParams(vmem_limit_bytes=48 * 1024 * 1024),
        cost_estimate=pl.CostEstimate(
            flops=exposures * (8 * ph * hin * window + 4 * ph * kw * width),
            transcendentals=0,
            bytes_accessed=exposures * hin * window * 6 + per * kw * tw * 2 + slots * 2 * RB * width * 2,
        ),
    )(weights, send_idx, images, masks, row_kernels, col_kernel)


def local(images, masks, row_kernels, col_kernel, inv_var, dest_col, dest_row):
    exposures = images.shape[1]
    tile_width = col_kernel.shape[2]
    cw = col_kernel.shape[0] * tile_width
    pw = cw - 2 * tile_width
    width = cw // CHUNKS
    first_exp = lax.axis_index("skyx") * exposures
    weights = lax.dynamic_slice_in_dim(inv_var[0], first_exp, exposures)

    slot_dest = dest_col[0, :, 0]
    slot_rows = dest_row[0]
    slot_count = slot_dest.shape[0]
    peers = lax.axis_size("skyx")
    capacity = max(2, (3 * slot_count + 2 * peers - 1) // (2 * peers))
    positions = (PR + 2 * OVY) // RB
    earlier = (jnp.arange(slot_count)[None, :] < jnp.arange(slot_count)[:, None]).astype(jnp.int32)
    onehot_dest = (slot_dest[:, None] == jnp.arange(peers)[None, :]).astype(jnp.int32)
    ranks = jnp.sum(jnp.dot(earlier, onehot_dest) * onehot_dest, axis=1)
    chosen = (slot_dest[None, None, :] == jnp.arange(peers)[:, None, None]) & (
        ranks[None, None, :] == jnp.arange(capacity)[None, :, None]
    )
    send_rows = jnp.sum(jnp.where(chosen, slot_rows[None, None, :] + 1, 0), axis=2) - 1
    send_idx = jnp.sum(jnp.where(chosen, jnp.arange(slot_count)[None, None, :] + 1, 0), axis=2) - 1
    send_idx = jnp.clip(send_idx, 0, slot_count - 1).reshape(-1)
    recv_rows = lax.all_to_all(send_rows, "skyx", split_axis=0, concat_axis=0, tiled=True)
    onehot_pos = (recv_rows.reshape(-1)[:, None] == jnp.arange(positions)[None, :]).astype(jnp.bfloat16)

    margin = OVY // RB
    inner = PR // RB
    interiors = []
    for chunk in range(CHUNKS):
        send_buf = warp_chunk(chunk, weights, send_idx, images, masks, row_kernels, col_kernel)
        send_buf = send_buf.reshape((peers, capacity) + send_buf.shape[1:])
        arrived = lax.all_to_all(send_buf, "skyx", split_axis=0, concat_axis=0, tiled=True)
        arrived = arrived.reshape((-1,) + arrived.shape[2:])
        canvas = jnp.einsum("sn,sprw->nprw", onehot_pos, arrived, preferred_element_type=jnp.float32)
        upper = canvas[:margin].astype(jnp.bfloat16)
        lower = canvas[margin + inner :].astype(jnp.bfloat16)
        from_above = shifted(lower, "skyy", 1).astype(jnp.float32)
        from_below = shifted(upper, "skyy", -1).astype(jnp.float32)
        interior = canvas[margin : margin + inner]
        interior = interior.at[:margin].add(from_above)
        interior = interior.at[inner - margin :].add(from_below)
        interiors.append(interior)

    left_part = interiors[0][..., :tile_width].astype(jnp.bfloat16)
    right_part = interiors[-1][..., width - tile_width :].astype(jnp.bfloat16)
    from_left = shifted(right_part, "skyx", 1).astype(jnp.float32)
    from_right = shifted(left_part, "skyx", -1).astype(jnp.float32)
    first = interiors[0][..., tile_width:]
    first = first.at[..., :tile_width].add(from_left)
    last = interiors[-1][..., : width - tile_width]
    last = last.at[..., width - 2 * tile_width :].add(from_right)
    core = jnp.concatenate([first] + interiors[1:-1] + [last], axis=-1)
    num = core[:, 0].reshape(PR, pw)
    den = core[:, 1].reshape(PR, pw)
    return num / jnp.maximum(den, 1.0)


def solution(mesh):
    in_specs = (
        P(("tract", "skyy"), "skyx", None, None),
        P(("tract", "skyy"), "skyx", None, None),
        P(("tract", "skyy"), "skyx", None, None),
        P("tract", None, None),
        P(("tract", "skyy"), None),
        P(("tract", "skyy"), "skyx", None),
        P(("tract", "skyy"), "skyx"),
    )
    out_specs = P(("tract", "skyy"), "skyx")
    return jax.shard_map(local, mesh=mesh, in_specs=in_specs, out_specs=out_specs, check_vma=False)
```

```python
import jax
import jax.numpy as jnp
from jax import lax
from jax.experimental import pallas as pl
from jax.experimental.pallas import tpu as pltpu
from jax.sharding import PartitionSpec as P

OVY = 64
PR = 128
RB = 8
CHUNKS = 3
ROW_PIECE = 640


def shifted(value, axis, steps):
    count = lax.axis_size(axis)
    first, last = (max(0, -steps), min(count, count - steps))
    return lax.ppermute(value, axis, [(source, source + steps) for source in range(first, last)])


def make_warp_kernel(start, width, exposures):
    def kernel(w_ref, idx_ref, img_hbm, mask_hbm, rk_ref, ck_ref, out_ref, img_buf, mask_buf, rw_buf, blk_buf, sems):
        ph = rk_ref.shape[2]
        tiles, kw, tw = ck_ref.shape
        blocks = ph // RB
        copies = []
        for e in range(exposures):
            ci = pltpu.make_async_copy(img_hbm.at[0, e, :, pl.ds(start, width)], img_buf.at[e], sems.at[0, e])
            cm = pltpu.make_async_copy(mask_hbm.at[0, e, :, pl.ds(start, width)], mask_buf.at[e], sems.at[1, e])
            ci.start()
            cm.start()
            copies.append((ci, cm))
        for e in range(exposures):
            ci, cm = copies[e]
            ci.wait()
            cm.wait()
            rk = rk_ref[0, e]
            piece_start = 0
            while piece_start < width:
                piece = min(ROW_PIECE, width - piece_start)
                cols = pl.ds(piece_start, piece)
                good = mask_buf[e, :, cols] == 0
                img = img_buf[e, :, cols]
                p0 = jnp.where(good, img, jnp.zeros_like(img))
                p1 = good.astype(jnp.bfloat16)
                rw_buf[0:ph, cols] = jnp.dot(rk, p0, preferred_element_type=jnp.float32).astype(jnp.bfloat16)
                rw_buf[ph : 2 * ph, cols] = jnp.dot(rk, p1, preferred_element_type=jnp.float32).astype(jnp.bfloat16)
                piece_start += piece
            weight = w_ref[e]

            def tile(t, carry):
                off = pl.multiple_of(t * tw, tw)
                x = rw_buf[:, pl.ds(off, kw)]
                r = jnp.dot(x, ck_ref[t], preferred_element_type=jnp.float32) * weight
                rows = pl.ds(e * blocks, blocks)
                blk_buf[rows, 0, :, pl.ds(off, tw)] = r[0:ph].reshape(blocks, RB, tw).astype(jnp.bfloat16)
                blk_buf[rows, 1, :, pl.ds(off, tw)] = r[ph : 2 * ph].reshape(blocks, RB, tw).astype(jnp.bfloat16)
                return carry

            lax.fori_loop(0, tiles, tile, 0)

        def gather(slot, carry):
            out_ref[slot] = blk_buf[idx_ref[slot]]
            return carry

        lax.fori_loop(0, out_ref.shape[0], gather, 0)

    return kernel


def warp_chunk(chunk, weights, send_idx, images, masks, row_kernels, col_kernel):
    _, exposures, hin, win = images.shape
    ph = row_kernels.shape[2]
    tiles, kw, tw = col_kernel.shape
    per = tiles // CHUNKS
    width = per * tw
    window = width + kw - tw
    start = chunk * width
    blocks = ph // RB
    slots = send_idx.shape[0]
    return pl.pallas_call(
        make_warp_kernel(start, window, exposures),
        grid=(1,),
        in_specs=[
            pl.BlockSpec(memory_space=pltpu.SMEM),
            pl.BlockSpec(memory_space=pltpu.SMEM),
            pl.BlockSpec(memory_space=pl.ANY),
            pl.BlockSpec(memory_space=pl.ANY),
            pl.BlockSpec(memory_space=pltpu.VMEM),
            pl.BlockSpec((per, kw, tw), lambda i: (chunk, 0, 0)),
        ],
        out_specs=pl.BlockSpec(memory_space=pltpu.VMEM),
        out_shape=jax.ShapeDtypeStruct((slots, 2, RB, width), jnp.bfloat16),
        scratch_shapes=[
            pltpu.VMEM((exposures, hin, window), jnp.bfloat16),
            pltpu.VMEM((exposures, hin, window), jnp.int32),
            pltpu.VMEM((2 * ph, window), jnp.bfloat16),
            pltpu.VMEM((exposures * blocks, 2, RB, width), jnp.bfloat16),
            pltpu.SemaphoreType.DMA((2, exposures)),
        ],
        compiler_params=pltpu.CompilerParams(vmem_limit_bytes=48 * 1024 * 1024),
        cost_estimate=pl.CostEstimate(
            flops=exposures * (8 * ph * hin * window + 4 * ph * kw * width),
            transcendentals=0,
            bytes_accessed=exposures * hin * window * 6 + per * kw * tw * 2 + slots * 2 * RB * width * 2,
        ),
    )(weights, send_idx, images, masks, row_kernels, col_kernel)


def make_place_kernel(groups, capacity, positions, margin, inner):
    def kernel(rows_ref, *refs):
        recv_refs = refs[:groups]
        upper_ref, lower_ref, int_ref, canvas = refs[groups:]
        canvas[...] = jnp.zeros(canvas.shape, jnp.float32)
        for g in range(groups):
            def body(c, carry, g=g):
                pos = rows_ref[g * capacity + c]

                @pl.when((pos >= 0) & (pos < positions))
                def _():
                    canvas[pos] += recv_refs[g][c].astype(jnp.float32)

                return carry

            lax.fori_loop(0, capacity, body, 0)
        upper_ref[...] = canvas[0:margin].astype(jnp.bfloat16)
        lower_ref[...] = canvas[margin + inner :].astype(jnp.bfloat16)
        int_ref[...] = canvas[margin : margin + inner]

    return kernel


def place(rows, recvs, positions, margin, inner):
    groups = len(recvs)
    capacity = recvs[0].shape[0]
    block = recvs[0].shape[1:]
    return pl.pallas_call(
        make_place_kernel(groups, capacity, positions, margin, inner),
        in_specs=[pl.BlockSpec(memory_space=pltpu.SMEM)] + [pl.BlockSpec(memory_space=pltpu.VMEM)] * groups,
        out_specs=[pl.BlockSpec(memory_space=pltpu.VMEM)] * 3,
        out_shape=[
            jax.ShapeDtypeStruct((margin,) + block, jnp.bfloat16),
            jax.ShapeDtypeStruct((margin,) + block, jnp.bfloat16),
            jax.ShapeDtypeStruct((inner,) + block, jnp.float32),
        ],
        scratch_shapes=[pltpu.VMEM((positions,) + block, jnp.float32)],
        compiler_params=pltpu.CompilerParams(vmem_limit_bytes=32 * 1024 * 1024),
    )(rows, *recvs)


def local(images, masks, row_kernels, col_kernel, inv_var, dest_col, dest_row):
    exposures = images.shape[1]
    tile_width = col_kernel.shape[2]
    cw = col_kernel.shape[0] * tile_width
    pw = cw - 2 * tile_width
    width = cw // CHUNKS
    first_exp = lax.axis_index("skyx") * exposures
    weights = lax.dynamic_slice_in_dim(inv_var[0], first_exp, exposures)

    slot_dest = dest_col[0, :, 0]
    slot_rows = dest_row[0]
    slot_count = slot_dest.shape[0]
    peers = lax.axis_size("skyx")
    capacity = max(2, (3 * slot_count + 2 * peers - 1) // (2 * peers))
    positions = (PR + 2 * OVY) // RB
    offsets = (slot_dest - lax.axis_index("skyx")) % peers
    earlier = (jnp.arange(slot_count)[None, :] < jnp.arange(slot_count)[:, None]).astype(jnp.int32)
    onehot_dest = (offsets[:, None] == jnp.arange(peers)[None, :]).astype(jnp.int32)
    ranks = jnp.sum(jnp.dot(earlier, onehot_dest) * onehot_dest, axis=1)
    chosen = (offsets[None, None, :] == jnp.arange(peers)[:, None, None]) & (
        ranks[None, None, :] == jnp.arange(capacity)[None, :, None]
    )
    send_rows = jnp.sum(jnp.where(chosen, slot_rows[None, None, :] + 1, 0), axis=2) - 1
    send_idx = jnp.sum(jnp.where(chosen, jnp.arange(slot_count)[None, None, :] + 1, 0), axis=2) - 1
    send_idx = jnp.clip(send_idx, 0, slot_count - 1).reshape(-1)
    rings = [[(i, (i + step) % peers) for i in range(peers)] for step in range(peers)]
    recv_rows = [send_rows[0]] + [lax.ppermute(send_rows[step], "skyx", rings[step]) for step in range(1, peers)]
    recv_rows = jnp.concatenate(recv_rows)

    margin = OVY // RB
    inner = PR // RB
    interiors = []
    for chunk in range(CHUNKS):
        send_buf = warp_chunk(chunk, weights, send_idx, images, masks, row_kernels, col_kernel)
        send_buf = send_buf.reshape((peers, capacity) + send_buf.shape[1:])
        recvs = [send_buf[0]] + [lax.ppermute(send_buf[step], "skyx", rings[step]) for step in range(1, peers)]
        upper, lower, interior = place(recv_rows, recvs, positions, margin, inner)
        from_above = shifted(lower, "skyy", 1).astype(jnp.float32)
        from_below = shifted(upper, "skyy", -1).astype(jnp.float32)
        interior = interior.at[:margin].add(from_above)
        interior = interior.at[inner - margin :].add(from_below)
        interiors.append(interior)

    left_part = interiors[0][..., :tile_width].astype(jnp.bfloat16)
    right_part = interiors[-1][..., width - tile_width :].astype(jnp.bfloat16)
    from_left = shifted(right_part, "skyx", 1).astype(jnp.float32)
    from_right = shifted(left_part, "skyx", -1).astype(jnp.float32)
    first = interiors[0][..., tile_width:]
    first = first.at[..., :tile_width].add(from_left)
    last = interiors[-1][..., : width - tile_width]
    last = last.at[..., width - 2 * tile_width :].add(from_right)
    core = jnp.concatenate([first] + interiors[1:-1] + [last], axis=-1)
    num = core[:, 0].reshape(PR, pw)
    den = core[:, 1].reshape(PR, pw)
    return num / jnp.maximum(den, 1.0)


def solution(mesh):
    in_specs = (
        P(("tract", "skyy"), "skyx", None, None),
        P(("tract", "skyy"), "skyx", None, None),
        P(("tract", "skyy"), "skyx", None, None),
        P("tract", None, None),
        P(("tract", "skyy"), None),
        P(("tract", "skyy"), "skyx", None),
        P(("tract", "skyy"), "skyx"),
    )
    out_specs = P(("tract", "skyy"), "skyx")
    return jax.shard_map(local, mesh=mesh, in_specs=in_specs, out_specs=out_specs, check_vma=False)
```

```python
import jax
import jax.numpy as jnp
from jax import lax
from jax.experimental import pallas as pl
from jax.experimental.pallas import tpu as pltpu
from jax.sharding import PartitionSpec as P

OVY = 64
PR = 128
RB = 8
CHUNKS = 3
ROW_PIECE = 640


def shifted(value, axis, steps):
    count = lax.axis_size(axis)
    first, last = (max(0, -steps), min(count, count - steps))
    return lax.ppermute(value, axis, [(source, source + steps) for source in range(first, last)])


def make_warp_kernel(start, width, exposures):
    def kernel(w_ref, idx_ref, img_hbm, mask_hbm, rk_ref, ck_ref, prev_ref, out_ref, img_buf, mask_buf, rw_buf, blk_buf, sems):
        ph = rk_ref.shape[2]
        tiles, kw, tw = ck_ref.shape
        blocks = ph // RB
        copies = []
        for e in range(exposures):
            ci = pltpu.make_async_copy(img_hbm.at[0, e, :, pl.ds(start, width)], img_buf.at[e], sems.at[0, e])
            cm = pltpu.make_async_copy(mask_hbm.at[0, e, :, pl.ds(start, width)], mask_buf.at[e], sems.at[1, e])
            ci.start()
            cm.start()
            copies.append((ci, cm))
        for e in range(exposures):
            ci, cm = copies[e]
            ci.wait()
            cm.wait()
            rk = rk_ref[0, e]
            piece_start = 0
            while piece_start < width:
                piece = min(ROW_PIECE, width - piece_start)
                cols = pl.ds(piece_start, piece)
                good = mask_buf[e, :, cols] == 0
                img = img_buf[e, :, cols]
                p0 = jnp.where(good, img, jnp.zeros_like(img))
                p1 = good.astype(jnp.bfloat16)
                rw_buf[0:ph, cols] = jnp.dot(rk, p0, preferred_element_type=jnp.float32).astype(jnp.bfloat16)
                rw_buf[ph : 2 * ph, cols] = jnp.dot(rk, p1, preferred_element_type=jnp.float32).astype(jnp.bfloat16)
                piece_start += piece
            weight = w_ref[e]

            def tile(t, carry):
                off = pl.multiple_of(t * tw, tw)
                x = rw_buf[:, pl.ds(off, kw)]
                r = jnp.dot(x, ck_ref[t], preferred_element_type=jnp.float32) * weight
                rows = pl.ds(e * blocks, blocks)
                blk_buf[rows, 0, :, pl.ds(off, tw)] = r[0:ph].reshape(blocks, RB, tw).astype(jnp.bfloat16)
                blk_buf[rows, 1, :, pl.ds(off, tw)] = r[ph : 2 * ph].reshape(blocks, RB, tw).astype(jnp.bfloat16)
                return carry

            lax.fori_loop(0, tiles, tile, 0)

        def gather(slot, carry):
            out_ref[slot] = blk_buf[idx_ref[slot]]
            return carry

        lax.fori_loop(0, out_ref.shape[0], gather, 0)

    return kernel


def warp_chunk(chunk, weights, send_idx, images, masks, row_kernels, col_kernel, previous):
    _, exposures, hin, win = images.shape
    ph = row_kernels.shape[2]
    tiles, kw, tw = col_kernel.shape
    per = tiles // CHUNKS
    width = per * tw
    window = width + kw - tw
    start = chunk * width
    blocks = ph // RB
    slots = send_idx.shape[0]
    return pl.pallas_call(
        make_warp_kernel(start, window, exposures),
        grid=(1,),
        in_specs=[
            pl.BlockSpec(memory_space=pltpu.SMEM),
            pl.BlockSpec(memory_space=pltpu.SMEM),
            pl.BlockSpec(memory_space=pl.ANY),
            pl.BlockSpec(memory_space=pl.ANY),
            pl.BlockSpec(memory_space=pltpu.VMEM),
            pl.BlockSpec((per, kw, tw), lambda i: (chunk, 0, 0)),
            pl.BlockSpec(memory_space=pl.ANY),
        ],
        out_specs=pl.BlockSpec(memory_space=pltpu.VMEM),
        out_shape=jax.ShapeDtypeStruct((slots, 2, RB, width), jnp.bfloat16),
        scratch_shapes=[
            pltpu.VMEM((exposures, hin, window), jnp.bfloat16),
            pltpu.VMEM((exposures, hin, window), jnp.int32),
            pltpu.VMEM((2 * ph, window), jnp.bfloat16),
            pltpu.VMEM((exposures * blocks, 2, RB, width), jnp.bfloat16),
            pltpu.SemaphoreType.DMA((2, exposures)),
        ],
        compiler_params=pltpu.CompilerParams(vmem_limit_bytes=48 * 1024 * 1024),
        cost_estimate=pl.CostEstimate(
            flops=exposures * (8 * ph * hin * window + 4 * ph * kw * width),
            transcendentals=0,
            bytes_accessed=exposures * hin * window * 6 + per * kw * tw * 2 + slots * 2 * RB * width * 2,
        ),
    )(weights, send_idx, images, masks, row_kernels, col_kernel, previous)


def make_place_kernel(groups, capacity, positions, margin, inner):
    def kernel(rows_ref, *refs):
        recv_refs = refs[:groups]
        upper_ref, lower_ref, int_ref, canvas = refs[-4:]
        canvas[...] = jnp.zeros(canvas.shape, jnp.float32)
        for g in range(groups):
            def body(c, carry, g=g):
                pos = rows_ref[g * capacity + c]

                @pl.when((pos >= 0) & (pos < positions))
                def _():
                    canvas[pos] += recv_refs[g][c].astype(jnp.float32)

                return carry

            lax.fori_loop(0, capacity, body, 0)
        upper_ref[...] = canvas[0:margin].astype(jnp.bfloat16)
        lower_ref[...] = canvas[margin + inner :].astype(jnp.bfloat16)
        int_ref[...] = canvas[margin : margin + inner]

    return kernel


def place(rows, recvs, after, positions, margin, inner):
    after = list(after)
    groups = len(recvs)
    capacity = recvs[0].shape[0]
    block = recvs[0].shape[1:]
    return pl.pallas_call(
        make_place_kernel(groups, capacity, positions, margin, inner),
        in_specs=[pl.BlockSpec(memory_space=pltpu.SMEM)]
        + [pl.BlockSpec(memory_space=pltpu.VMEM)] * groups
        + [pl.BlockSpec(memory_space=pl.ANY)] * len(after),
        out_specs=[pl.BlockSpec(memory_space=pltpu.VMEM)] * 3,
        out_shape=[
            jax.ShapeDtypeStruct((margin,) + block, jnp.bfloat16),
            jax.ShapeDtypeStruct((margin,) + block, jnp.bfloat16),
            jax.ShapeDtypeStruct((inner,) + block, jnp.float32),
        ],
        scratch_shapes=[pltpu.VMEM((positions,) + block, jnp.float32)],
        compiler_params=pltpu.CompilerParams(vmem_limit_bytes=32 * 1024 * 1024),
    )(rows, *recvs, *after)


def local(images, masks, row_kernels, col_kernel, inv_var, dest_col, dest_row):
    exposures = images.shape[1]
    tile_width = col_kernel.shape[2]
    cw = col_kernel.shape[0] * tile_width
    pw = cw - 2 * tile_width
    width = cw // CHUNKS
    first_exp = lax.axis_index("skyx") * exposures
    weights = lax.dynamic_slice_in_dim(inv_var[0], first_exp, exposures)

    slot_dest = dest_col[0, :, 0]
    slot_rows = dest_row[0]
    slot_count = slot_dest.shape[0]
    peers = lax.axis_size("skyx")
    capacity = max(2, (3 * slot_count + 2 * peers - 1) // (2 * peers))
    positions = (PR + 2 * OVY) // RB
    offsets = (slot_dest - lax.axis_index("skyx")) % peers
    earlier = (jnp.arange(slot_count)[None, :] < jnp.arange(slot_count)[:, None]).astype(jnp.int32)
    onehot_dest = (offsets[:, None] == jnp.arange(peers)[None, :]).astype(jnp.int32)
    ranks = jnp.sum(jnp.dot(earlier, onehot_dest) * onehot_dest, axis=1)
    chosen = (offsets[None, None, :] == jnp.arange(peers)[:, None, None]) & (
        ranks[None, None, :] == jnp.arange(capacity)[None, :, None]
    )
    send_rows = jnp.sum(jnp.where(chosen, slot_rows[None, None, :] + 1, 0), axis=2) - 1
    send_idx = jnp.sum(jnp.where(chosen, jnp.arange(slot_count)[None, None, :] + 1, 0), axis=2) - 1
    send_idx = jnp.clip(send_idx, 0, slot_count - 1).reshape(-1)
    rings = [[(i, (i + step) % peers) for i in range(peers)] for step in range(peers)]
    table = lax.all_gather(jnp.stack([slot_dest, slot_rows]), "skyx")
    mine = (table[:, 0] == lax.axis_index("skyx")).astype(jnp.int32)
    mine_rank = jnp.dot(mine, earlier.T)
    picked = (mine[:, None, :] == 1) & (mine_rank[:, None, :] == jnp.arange(capacity)[None, :, None])
    recv_from = jnp.sum(jnp.where(picked, table[:, 1][:, None, :] + 1, 0), axis=2)
    sources = (lax.axis_index("skyx") - jnp.arange(peers)) % peers
    by_step = sources[:, None] == jnp.arange(peers)[None, :]
    recv_rows = jnp.sum(jnp.where(by_step[:, :, None], recv_from[None, :, :], 0), axis=1) - 1
    recv_rows = recv_rows.reshape(-1)

    margin = OVY // RB
    inner = PR // RB
    interiors = []
    after = [recv_rows]
    previous = recv_rows
    for chunk in range(CHUNKS):
        send_buf = warp_chunk(chunk, weights, send_idx, images, masks, row_kernels, col_kernel, previous)
        previous = send_buf
        send_buf = send_buf.reshape((peers, capacity) + send_buf.shape[1:])
        recvs = [send_buf[0]] + [lax.ppermute(send_buf[step], "skyx", rings[step]) for step in range(1, peers)]
        upper, lower, interior = place(recv_rows, recvs, after, positions, margin, inner)
        from_above = shifted(lower, "skyy", 1).astype(jnp.float32)
        from_below = shifted(upper, "skyy", -1).astype(jnp.float32)
        after = [from_above, from_below]
        interior = interior.at[:margin].add(from_above)
        interior = interior.at[inner - margin :].add(from_below)
        interiors.append(interior)

    left_part = interiors[0][..., :tile_width].astype(jnp.bfloat16)
    right_part = interiors[-1][..., width - tile_width :].astype(jnp.bfloat16)
    from_left = shifted(right_part, "skyx", 1).astype(jnp.float32)
    from_right = shifted(left_part, "skyx", -1).astype(jnp.float32)
    first = interiors[0][..., tile_width:]
    first = first.at[..., :tile_width].add(from_left)
    last = interiors[-1][..., : width - tile_width]
    last = last.at[..., width - 2 * tile_width :].add(from_right)
    core = jnp.concatenate([first] + interiors[1:-1] + [last], axis=-1)
    num = core[:, 0].reshape(PR, pw)
    den = core[:, 1].reshape(PR, pw)
    return num / jnp.maximum(den, 1.0)


def solution(mesh):
    in_specs = (
        P(("tract", "skyy"), "skyx", None, None),
        P(("tract", "skyy"), "skyx", None, None),
        P(("tract", "skyy"), "skyx", None, None),
        P("tract", None, None),
        P(("tract", "skyy"), None),
        P(("tract", "skyy"), "skyx", None),
        P(("tract", "skyy"), "skyx"),
    )
    out_specs = P(("tract", "skyy"), "skyx")
    return jax.shard_map(local, mesh=mesh, in_specs=in_specs, out_specs=out_specs, check_vma=False)
```

```python
import jax
import jax.numpy as jnp
from jax import lax
from jax.experimental import pallas as pl
from jax.experimental.pallas import tpu as pltpu
from jax.sharding import PartitionSpec as P

OVY = 64
PR = 128
RB = 8
SPLIT = (5, 11, 11, 6)
ROW_PIECE = 640


def shifted(value, axis, steps):
    count = lax.axis_size(axis)
    first, last = (max(0, -steps), min(count, count - steps))
    return lax.ppermute(value, axis, [(source, source + steps) for source in range(first, last)])


def make_warp_kernel(start, width, first_tile, exposures):
    def kernel(w_ref, idx_ref, img_hbm, mask_hbm, rk_ref, ck_hbm, prev_ref, out_ref, img_buf, mask_buf, rw_buf, blk_buf, ck_ref, sems):
        ph = rk_ref.shape[2]
        tiles, kw, tw = ck_ref.shape
        blocks = ph // RB
        ck_copy = pltpu.make_async_copy(ck_hbm.at[pl.ds(first_tile, tiles)], ck_ref, sems.at[2, 0])
        ck_copy.start()
        copies = []
        for e in range(exposures):
            ci = pltpu.make_async_copy(img_hbm.at[0, e, :, pl.ds(start, width)], img_buf.at[e], sems.at[0, e])
            cm = pltpu.make_async_copy(mask_hbm.at[0, e, :, pl.ds(start, width)], mask_buf.at[e], sems.at[1, e])
            ci.start()
            cm.start()
            copies.append((ci, cm))
        for e in range(exposures):
            ci, cm = copies[e]
            ci.wait()
            cm.wait()
            rk = rk_ref[0, e]
            if e == 0:
                ck_copy.wait()
            piece_start = 0
            while piece_start < width:
                piece = min(ROW_PIECE, width - piece_start)
                cols = pl.ds(piece_start, piece)
                good = mask_buf[e, :, cols] == 0
                img = img_buf[e, :, cols]
                p0 = jnp.where(good, img, jnp.zeros_like(img))
                p1 = good.astype(jnp.bfloat16)
                rw_buf[0:ph, cols] = jnp.dot(rk, p0, preferred_element_type=jnp.float32).astype(jnp.bfloat16)
                rw_buf[ph : 2 * ph, cols] = jnp.dot(rk, p1, preferred_element_type=jnp.float32).astype(jnp.bfloat16)
                piece_start += piece
            weight = w_ref[e]

            def tile(t, carry):
                off = pl.multiple_of(t * tw, tw)
                x = rw_buf[:, pl.ds(off, kw)]
                r = jnp.dot(x, ck_ref[t], preferred_element_type=jnp.float32) * weight
                rows = pl.ds(e * blocks, blocks)
                blk_buf[rows, 0, :, pl.ds(off, tw)] = r[0:ph].reshape(blocks, RB, tw).astype(jnp.bfloat16)
                blk_buf[rows, 1, :, pl.ds(off, tw)] = r[ph : 2 * ph].reshape(blocks, RB, tw).astype(jnp.bfloat16)
                return carry

            lax.fori_loop(0, tiles, tile, 0)

        def gather(slot, carry):
            out_ref[slot] = blk_buf[idx_ref[slot]]
            return carry

        lax.fori_loop(0, out_ref.shape[0], gather, 0)

    return kernel


def warp_chunk(first_tile, per, weights, send_idx, images, masks, row_kernels, col_kernel, previous):
    _, exposures, hin, win = images.shape
    ph = row_kernels.shape[2]
    tiles, kw, tw = col_kernel.shape
    width = per * tw
    window = width + kw - tw
    start = first_tile * tw
    blocks = ph // RB
    slots = send_idx.shape[0]
    return pl.pallas_call(
        make_warp_kernel(start, window, first_tile, exposures),
        in_specs=[
            pl.BlockSpec(memory_space=pltpu.SMEM),
            pl.BlockSpec(memory_space=pltpu.SMEM),
            pl.BlockSpec(memory_space=pl.ANY),
            pl.BlockSpec(memory_space=pl.ANY),
            pl.BlockSpec(memory_space=pltpu.VMEM),
            pl.BlockSpec(memory_space=pl.ANY),
            pl.BlockSpec(memory_space=pl.ANY),
        ],
        out_specs=pl.BlockSpec(memory_space=pltpu.VMEM),
        out_shape=jax.ShapeDtypeStruct((slots, 2, RB, width), jnp.bfloat16),
        scratch_shapes=[
            pltpu.VMEM((exposures, hin, window), jnp.bfloat16),
            pltpu.VMEM((exposures, hin, window), jnp.int32),
            pltpu.VMEM((2 * ph, window), jnp.bfloat16),
            pltpu.VMEM((exposures * blocks, 2, RB, width), jnp.bfloat16),
            pltpu.VMEM((per, kw, tw), jnp.bfloat16),
            pltpu.SemaphoreType.DMA((3, exposures)),
        ],
        compiler_params=pltpu.CompilerParams(vmem_limit_bytes=48 * 1024 * 1024),
        cost_estimate=pl.CostEstimate(
            flops=exposures * (8 * ph * hin * window + 4 * ph * kw * width),
            transcendentals=0,
            bytes_accessed=exposures * hin * window * 6 + per * kw * tw * 2 + slots * 2 * RB * width * 2,
        ),
    )(weights, send_idx, images, masks, row_kernels, col_kernel, previous)


def make_place_kernel(groups, capacity, positions, margin, inner):
    def kernel(rows_ref, *refs):
        recv_refs = refs[:groups]
        upper_ref, lower_ref, int_ref, canvas = refs[-4:]
        canvas[...] = jnp.zeros(canvas.shape, jnp.float32)
        for g in range(groups):
            def body(c, carry, g=g):
                pos = rows_ref[g * capacity + c]

                @pl.when((pos >= 0) & (pos < positions))
                def _():
                    canvas[pos] += recv_refs[g][c].astype(jnp.float32)

                return carry

            lax.fori_loop(0, capacity, body, 0)
        upper_ref[...] = canvas[0:margin].astype(jnp.bfloat16)
        lower_ref[...] = canvas[margin + inner :].astype(jnp.bfloat16)
        int_ref[...] = canvas[margin : margin + inner]

    return kernel


def place(rows, recvs, after, positions, margin, inner):
    after = list(after)
    groups = len(recvs)
    capacity = recvs[0].shape[0]
    block = recvs[0].shape[1:]
    return pl.pallas_call(
        make_place_kernel(groups, capacity, positions, margin, inner),
        in_specs=[pl.BlockSpec(memory_space=pltpu.SMEM)]
        + [pl.BlockSpec(memory_space=pltpu.VMEM)] * groups
        + [pl.BlockSpec(memory_space=pl.ANY)] * len(after),
        out_specs=[pl.BlockSpec(memory_space=pltpu.VMEM)] * 3,
        out_shape=[
            jax.ShapeDtypeStruct((margin,) + block, jnp.bfloat16),
            jax.ShapeDtypeStruct((margin,) + block, jnp.bfloat16),
            jax.ShapeDtypeStruct((inner,) + block, jnp.float32),
        ],
        scratch_shapes=[pltpu.VMEM((positions,) + block, jnp.float32)],
        compiler_params=pltpu.CompilerParams(vmem_limit_bytes=32 * 1024 * 1024),
    )(rows, *recvs, *after)


def local(images, masks, row_kernels, col_kernel, inv_var, dest_col, dest_row):
    exposures = images.shape[1]
    tile_width = col_kernel.shape[2]
    cw = col_kernel.shape[0] * tile_width
    pw = cw - 2 * tile_width
    tiles = col_kernel.shape[0]
    bounds = [tiles * sum(SPLIT[:i]) // sum(SPLIT) for i in range(len(SPLIT) + 1)]
    first_exp = lax.axis_index("skyx") * exposures
    weights = lax.dynamic_slice_in_dim(inv_var[0], first_exp, exposures)

    slot_dest = dest_col[0, :, 0]
    slot_rows = dest_row[0]
    slot_count = slot_dest.shape[0]
    peers = lax.axis_size("skyx")
    capacity = max(2, (3 * slot_count + 2 * peers - 1) // (2 * peers))
    positions = (PR + 2 * OVY) // RB
    offsets = (slot_dest - lax.axis_index("skyx")) % peers
    earlier = (jnp.arange(slot_count)[None, :] < jnp.arange(slot_count)[:, None]).astype(jnp.int32)
    onehot_dest = (offsets[:, None] == jnp.arange(peers)[None, :]).astype(jnp.int32)
    ranks = jnp.sum(jnp.dot(earlier, onehot_dest) * onehot_dest, axis=1)
    chosen = (offsets[None, None, :] == jnp.arange(peers)[:, None, None]) & (
        ranks[None, None, :] == jnp.arange(capacity)[None, :, None]
    )
    send_rows = jnp.sum(jnp.where(chosen, slot_rows[None, None, :] + 1, 0), axis=2) - 1
    send_idx = jnp.sum(jnp.where(chosen, jnp.arange(slot_count)[None, None, :] + 1, 0), axis=2) - 1
    send_idx = jnp.clip(send_idx, 0, slot_count - 1).reshape(-1)
    rings = [[(i, (i + step) % peers) for i in range(peers)] for step in range(peers)]
    table = lax.all_gather(jnp.stack([slot_dest, slot_rows]), "skyx")
    mine = (table[:, 0] == lax.axis_index("skyx")).astype(jnp.int32)
    mine_rank = jnp.dot(mine, earlier.T)
    picked = (mine[:, None, :] == 1) & (mine_rank[:, None, :] == jnp.arange(capacity)[None, :, None])
    recv_from = jnp.sum(jnp.where(picked, table[:, 1][:, None, :] + 1, 0), axis=2)
    sources = (lax.axis_index("skyx") - jnp.arange(peers)) % peers
    by_step = sources[:, None] == jnp.arange(peers)[None, :]
    recv_rows = jnp.sum(jnp.where(by_step[:, :, None], recv_from[None, :, :], 0), axis=1) - 1
    recv_rows = recv_rows.reshape(-1)

    margin = OVY // RB
    inner = PR // RB
    interiors = []
    after = [recv_rows]
    previous = recv_rows
    for chunk in range(len(SPLIT)):
        per = bounds[chunk + 1] - bounds[chunk]
        send_buf = warp_chunk(bounds[chunk], per, weights, send_idx, images, masks, row_kernels, col_kernel, previous)
        previous = send_buf
        send_buf = send_buf.reshape((peers, capacity) + send_buf.shape[1:])
        recvs = [send_buf[0]] + [lax.ppermute(send_buf[step], "skyx", rings[step]) for step in range(1, peers)]
        upper, lower, interior = place(recv_rows, recvs, after, positions, margin, inner)
        from_above = shifted(lower, "skyy", 1).astype(jnp.float32)
        from_below = shifted(upper, "skyy", -1).astype(jnp.float32)
        after = [from_above, from_below]
        interior = interior.at[:margin].add(from_above)
        interior = interior.at[inner - margin :].add(from_below)
        interiors.append(interior)

    left_part = interiors[0][..., :tile_width].astype(jnp.bfloat16)
    width = interiors[-1].shape[-1]
    right_part = interiors[-1][..., width - tile_width :].astype(jnp.bfloat16)
    from_left = shifted(right_part, "skyx", 1).astype(jnp.float32)
    from_right = shifted(left_part, "skyx", -1).astype(jnp.float32)
    first = interiors[0][..., tile_width:]
    first = first.at[..., :tile_width].add(from_left)
    last = interiors[-1][..., : width - tile_width]
    last = last.at[..., width - 2 * tile_width :].add(from_right)
    core = jnp.concatenate([first] + interiors[1:-1] + [last], axis=-1)
    num = core[:, 0].reshape(PR, pw)
    den = core[:, 1].reshape(PR, pw)
    return num / jnp.maximum(den, 1.0)


def solution(mesh):
    in_specs = (
        P(("tract", "skyy"), "skyx", None, None),
        P(("tract", "skyy"), "skyx", None, None),
        P(("tract", "skyy"), "skyx", None, None),
        P("tract", None, None),
        P(("tract", "skyy"), None),
        P(("tract", "skyy"), "skyx", None),
        P(("tract", "skyy"), "skyx"),
    )
    out_specs = P(("tract", "skyy"), "skyx")
    return jax.shard_map(local, mesh=mesh, in_specs=in_specs, out_specs=out_specs, check_vma=False)
```

```python
import jax
import jax.numpy as jnp
from jax import lax
from jax.experimental import pallas as pl
from jax.experimental.pallas import tpu as pltpu
from jax.sharding import PartitionSpec as P


OVY = 64
PR = 128
RB = 8
SPLIT = (5, 11, 11, 6)
ROW_PIECE = 640


def shifted(value, axis, steps):
    count = lax.axis_size(axis)
    first, last = (max(0, -steps), min(count, count - steps))
    return lax.ppermute(value, axis, [(source, source + steps) for source in range(first, last)])


def make_warp_kernel(start, width, first_tile, exposures):
    def kernel(w_ref, idx_ref, img_hbm, mask_hbm, rk_ref, ck_hbm, prev_ref, out_ref, img_buf, mask_buf, rw_buf, blk_buf, ck_ref, sems):
        ph = rk_ref.shape[2]
        tiles, kw, tw = ck_ref.shape
        blocks = ph // RB
        ck_copy = pltpu.make_async_copy(ck_hbm.at[pl.ds(first_tile, tiles)], ck_ref, sems.at[2, 0])
        ck_copy.start()
        copies = []
        for e in range(exposures):
            ci = pltpu.make_async_copy(img_hbm.at[0, e, :, pl.ds(start, width)], img_buf.at[e], sems.at[0, e])
            cm = pltpu.make_async_copy(mask_hbm.at[0, e, :, pl.ds(start, width)], mask_buf.at[e], sems.at[1, e])
            ci.start()
            cm.start()
            copies.append((ci, cm))
        for e in range(exposures):
            ci, cm = copies[e]
            ci.wait()
            cm.wait()
            rk = rk_ref[0, e]
            if e == 0:
                ck_copy.wait()
            piece_start = 0
            while piece_start < width:
                piece = min(ROW_PIECE, width - piece_start)
                cols = pl.ds(piece_start, piece)
                good = mask_buf[e, :, cols] == 0
                img = img_buf[e, :, cols]
                p0 = jnp.where(good, img, jnp.zeros_like(img))
                p1 = good.astype(jnp.bfloat16)
                rw_buf[0:ph, cols] = jnp.dot(rk, p0, preferred_element_type=jnp.float32).astype(jnp.bfloat16)
                rw_buf[ph : 2 * ph, cols] = jnp.dot(rk, p1, preferred_element_type=jnp.float32).astype(jnp.bfloat16)
                piece_start += piece
            weight = w_ref[e]

            def tile(t, carry):
                off = pl.multiple_of(t * tw, tw)
                x = rw_buf[:, pl.ds(off, kw)]
                r = jnp.dot(x, ck_ref[t], preferred_element_type=jnp.float32) * weight
                rows = pl.ds(e * blocks, blocks)
                blk_buf[rows, 0, :, pl.ds(off, tw)] = r[0:ph].reshape(blocks, RB, tw).astype(jnp.bfloat16)
                blk_buf[rows, 1, :, pl.ds(off, tw)] = r[ph : 2 * ph].reshape(blocks, RB, tw).astype(jnp.bfloat16)
                return carry

            lax.fori_loop(0, tiles, tile, 0)

        def gather(slot, carry):
            out_ref[slot] = blk_buf[idx_ref[slot]]
            return carry

        lax.fori_loop(0, out_ref.shape[0], gather, 0)

    return kernel


def warp_chunk(first_tile, per, weights, send_idx, images, masks, row_kernels, col_kernel, previous):
    _, exposures, hin, _ = images.shape
    ph = row_kernels.shape[2]
    _, kw, tw = col_kernel.shape
    width = per * tw
    window = width + kw - tw
    start = first_tile * tw
    blocks = ph // RB
    slots = send_idx.shape[0]
    return pl.pallas_call(
        make_warp_kernel(start, window, first_tile, exposures),
        in_specs=[
            pl.BlockSpec(memory_space=pltpu.SMEM),
            pl.BlockSpec(memory_space=pltpu.SMEM),
            pl.BlockSpec(memory_space=pl.ANY),
            pl.BlockSpec(memory_space=pl.ANY),
            pl.BlockSpec(memory_space=pltpu.VMEM),
            pl.BlockSpec(memory_space=pl.ANY),
            pl.BlockSpec(memory_space=pl.ANY),
        ],
        out_specs=pl.BlockSpec(memory_space=pltpu.VMEM),
        out_shape=jax.ShapeDtypeStruct((slots, 2, RB, width), jnp.bfloat16),
        scratch_shapes=[
            pltpu.VMEM((exposures, hin, window), jnp.bfloat16),
            pltpu.VMEM((exposures, hin, window), jnp.int32),
            pltpu.VMEM((2 * ph, window), jnp.bfloat16),
            pltpu.VMEM((exposures * blocks, 2, RB, width), jnp.bfloat16),
            pltpu.VMEM((per, kw, tw), jnp.bfloat16),
            pltpu.SemaphoreType.DMA((3, exposures)),
        ],
        compiler_params=pltpu.CompilerParams(vmem_limit_bytes=48 * 1024 * 1024),
        cost_estimate=pl.CostEstimate(
            flops=exposures * (8 * ph * hin * window + 4 * ph * kw * width),
            transcendentals=0,
            bytes_accessed=exposures * hin * window * 6 + per * kw * tw * 2 + slots * 2 * RB * width * 2,
        ),
    )(weights, send_idx, images, masks, row_kernels, col_kernel, previous)


def make_place_kernel(groups, capacity, positions, margin, inner):
    def kernel(rows_ref, *refs):
        recv_refs = refs[:groups]
        upper_ref, lower_ref, int_ref, canvas = refs[-4:]
        canvas[...] = jnp.zeros(canvas.shape, jnp.float32)
        for g in range(groups):
            def body(c, carry, g=g):
                pos = rows_ref[g * capacity + c]

                @pl.when((pos >= 0) & (pos < positions))
                def _():
                    canvas[pos] += recv_refs[g][c].astype(jnp.float32)

                return carry

            lax.fori_loop(0, capacity, body, 0)
        upper_ref[...] = canvas[0:margin].astype(jnp.bfloat16)
        lower_ref[...] = canvas[margin + inner :].astype(jnp.bfloat16)
        int_ref[...] = canvas[margin : margin + inner]

    return kernel


def place(rows, recvs, after, positions, margin, inner):
    after = list(after)
    groups = len(recvs)
    capacity = recvs[0].shape[0]
    block = recvs[0].shape[1:]
    return pl.pallas_call(
        make_place_kernel(groups, capacity, positions, margin, inner),
        in_specs=[pl.BlockSpec(memory_space=pltpu.SMEM)]
        + [pl.BlockSpec(memory_space=pltpu.VMEM)] * groups
        + [pl.BlockSpec(memory_space=pl.ANY)] * len(after),
        out_specs=[pl.BlockSpec(memory_space=pltpu.VMEM)] * 3,
        out_shape=[
            jax.ShapeDtypeStruct((margin,) + block, jnp.bfloat16),
            jax.ShapeDtypeStruct((margin,) + block, jnp.bfloat16),
            jax.ShapeDtypeStruct((inner,) + block, jnp.float32),
        ],
        scratch_shapes=[pltpu.VMEM((positions,) + block, jnp.float32)],
        compiler_params=pltpu.CompilerParams(vmem_limit_bytes=32 * 1024 * 1024),
    )(rows, *recvs, *after)


def local_body(images, masks, row_kernels, col_kernel, inv_var, dest_col, dest_row):
    exposures = images.shape[1]
    tile_width = col_kernel.shape[2]
    cw = col_kernel.shape[0] * tile_width
    pw = cw - 2 * tile_width
    tiles = col_kernel.shape[0]
    bounds = [tiles * sum(SPLIT[:i]) // sum(SPLIT) for i in range(len(SPLIT) + 1)]
    first_exp = lax.axis_index("skyx") * exposures
    weights = lax.dynamic_slice_in_dim(inv_var[0], first_exp, exposures)

    slot_dest = dest_col[0, :, 0]
    slot_rows = dest_row[0]
    slot_count = slot_dest.shape[0]
    peers = lax.axis_size("skyx")
    capacity = max(2, (3 * slot_count + 2 * peers - 1) // (2 * peers))
    positions = (PR + 2 * OVY) // RB
    offsets = (slot_dest - lax.axis_index("skyx")) % peers
    earlier = (jnp.arange(slot_count)[None, :] < jnp.arange(slot_count)[:, None]).astype(jnp.int32)
    onehot_dest = (offsets[:, None] == jnp.arange(peers)[None, :]).astype(jnp.int32)
    ranks = jnp.sum(jnp.dot(earlier, onehot_dest) * onehot_dest, axis=1)
    chosen = (offsets[None, None, :] == jnp.arange(peers)[:, None, None]) & (
        ranks[None, None, :] == jnp.arange(capacity)[None, :, None]
    )
    send_rows = jnp.sum(jnp.where(chosen, slot_rows[None, None, :] + 1, 0), axis=2) - 1
    send_idx = jnp.sum(jnp.where(chosen, jnp.arange(slot_count)[None, None, :] + 1, 0), axis=2) - 1
    send_idx = jnp.clip(send_idx, 0, slot_count - 1).reshape(-1)
    rings = [[(i, (i + step) % peers) for i in range(peers)] for step in range(peers)]
    table = lax.all_gather(jnp.stack([slot_dest, slot_rows]), "skyx")
    mine = (table[:, 0] == lax.axis_index("skyx")).astype(jnp.int32)
    mine_rank = jnp.dot(mine, earlier.T)
    picked = (mine[:, None, :] == 1) & (mine_rank[:, None, :] == jnp.arange(capacity)[None, :, None])
    recv_from = jnp.sum(jnp.where(picked, table[:, 1][:, None, :] + 1, 0), axis=2)
    sources = (lax.axis_index("skyx") - jnp.arange(peers)) % peers
    by_step = sources[:, None] == jnp.arange(peers)[None, :]
    recv_rows = jnp.sum(jnp.where(by_step[:, :, None], recv_from[None, :, :], 0), axis=1) - 1
    recv_rows = recv_rows.reshape(-1)

    margin = OVY // RB
    inner = PR // RB
    interiors = []
    after = [recv_rows]
    previous = recv_rows
    for chunk in range(len(SPLIT)):
        per = bounds[chunk + 1] - bounds[chunk]
        send_buf = warp_chunk(bounds[chunk], per, weights, send_idx, images, masks, row_kernels, col_kernel, previous)
        previous = send_buf
        send_buf = send_buf.reshape((peers, capacity) + send_buf.shape[1:])
        recvs = [send_buf[0]] + [lax.ppermute(send_buf[step], "skyx", rings[step]) for step in range(1, peers)]
        upper, lower, interior = place(recv_rows, recvs, after, positions, margin, inner)
        from_above = shifted(lower, "skyy", 1)
        from_below = shifted(upper, "skyy", -1)
        from_above = from_above.astype(jnp.float32)
        from_below = from_below.astype(jnp.float32)
        after = [upper]
        interior = interior.at[:margin].add(from_above)
        interior = interior.at[inner - margin :].add(from_below)
        interiors.append(interior)

    left_part = interiors[0][..., :tile_width].astype(jnp.bfloat16)
    width = interiors[-1].shape[-1]
    right_part = interiors[-1][..., width - tile_width :].astype(jnp.bfloat16)
    from_left = shifted(right_part, "skyx", 1).astype(jnp.float32)
    from_right = shifted(left_part, "skyx", -1).astype(jnp.float32)
    first = interiors[0][..., tile_width:]
    first = first.at[..., :tile_width].add(from_left)
    last = interiors[-1][..., : width - tile_width]
    last = last.at[..., width - 2 * tile_width :].add(from_right)
    core = jnp.concatenate([first] + interiors[1:-1] + [last], axis=-1)
    num = core[:, 0].reshape(PR, pw)
    den = core[:, 1].reshape(PR, pw)
    return num / jnp.maximum(den, 1.0)


def solution(mesh):
    in_specs = (
        P(("tract", "skyy"), "skyx", None, None),
        P(("tract", "skyy"), "skyx", None, None),
        P(("tract", "skyy"), "skyx", None, None),
        P("tract", None, None),
        P(("tract", "skyy"), None),
        P(("tract", "skyy"), "skyx", None),
        P(("tract", "skyy"), "skyx"),
    )
    out_specs = P(("tract", "skyy"), "skyx")
    return jax.shard_map(local_body, mesh=mesh, in_specs=in_specs, out_specs=out_specs, check_vma=False)
```

```python
import jax
import jax.numpy as jnp
from jax import lax
from jax.experimental import pallas as pl
from jax.experimental.pallas import tpu as pltpu
from jax.sharding import PartitionSpec as P


OVY = 64
PR = 128
RB = 8
SPLIT = (5, 14, 6, 8)
ORDER = (0, 3, 1, 2)
ROW_PIECE = 640


def shifted(value, axis, steps):
    count = lax.axis_size(axis)
    first, last = (max(0, -steps), min(count, count - steps))
    return lax.ppermute(value, axis, [(source, source + steps) for source in range(first, last)])


def make_warp_kernel(start, width, first_tile, exposures):
    def kernel(w_ref, idx_ref, img_hbm, mask_hbm, rk_ref, ck_hbm, prev_ref, out_ref, img_buf, mask_buf, rw_buf, blk_buf, ck_ref, sems):
        ph = rk_ref.shape[2]
        tiles, kw, tw = ck_ref.shape
        blocks = ph // RB
        ck_copy = pltpu.make_async_copy(ck_hbm.at[pl.ds(first_tile, tiles)], ck_ref, sems.at[2, 0])
        ck_copy.start()
        copies = []
        for e in range(exposures):
            ci = pltpu.make_async_copy(img_hbm.at[0, e, :, pl.ds(start, width)], img_buf.at[e], sems.at[0, e])
            cm = pltpu.make_async_copy(mask_hbm.at[0, e, :, pl.ds(start, width)], mask_buf.at[e], sems.at[1, e])
            ci.start()
            cm.start()
            copies.append((ci, cm))
        for e in range(exposures):
            ci, cm = copies[e]
            ci.wait()
            cm.wait()
            rk = rk_ref[0, e]
            if e == 0:
                ck_copy.wait()
            piece_start = 0
            while piece_start < width:
                piece = min(ROW_PIECE, width - piece_start)
                cols = pl.ds(piece_start, piece)
                good = mask_buf[e, :, cols] == 0
                img = img_buf[e, :, cols]
                p0 = jnp.where(good, img, jnp.zeros_like(img))
                p1 = good.astype(jnp.bfloat16)
                rw_buf[0:ph, cols] = jnp.dot(rk, p0, preferred_element_type=jnp.float32).astype(jnp.bfloat16)
                rw_buf[ph : 2 * ph, cols] = jnp.dot(rk, p1, preferred_element_type=jnp.float32).astype(jnp.bfloat16)
                piece_start += piece
            weight = w_ref[e]

            def tile(t, carry):
                off = pl.multiple_of(t * tw, tw)
                x = rw_buf[:, pl.ds(off, kw)]
                r = jnp.dot(x, ck_ref[t], preferred_element_type=jnp.float32) * weight
                rows = pl.ds(e * blocks, blocks)
                blk_buf[rows, 0, :, pl.ds(off, tw)] = r[0:ph].reshape(blocks, RB, tw).astype(jnp.bfloat16)
                blk_buf[rows, 1, :, pl.ds(off, tw)] = r[ph : 2 * ph].reshape(blocks, RB, tw).astype(jnp.bfloat16)
                return carry

            lax.fori_loop(0, tiles, tile, 0)

        def gather(slot, carry):
            out_ref[slot] = blk_buf[idx_ref[slot]]
            return carry

        lax.fori_loop(0, out_ref.shape[0], gather, 0)

    return kernel


def warp_chunk(first_tile, per, weights, send_idx, images, masks, row_kernels, col_kernel, previous):
    _, exposures, hin, _ = images.shape
    ph = row_kernels.shape[2]
    _, kw, tw = col_kernel.shape
    width = per * tw
    window = width + kw - tw
    start = first_tile * tw
    blocks = ph // RB
    slots = send_idx.shape[0]
    return pl.pallas_call(
        make_warp_kernel(start, window, first_tile, exposures),
        in_specs=[
            pl.BlockSpec(memory_space=pltpu.SMEM),
            pl.BlockSpec(memory_space=pltpu.SMEM),
            pl.BlockSpec(memory_space=pl.ANY),
            pl.BlockSpec(memory_space=pl.ANY),
            pl.BlockSpec(memory_space=pltpu.VMEM),
            pl.BlockSpec(memory_space=pl.ANY),
            pl.BlockSpec(memory_space=pl.ANY),
        ],
        out_specs=pl.BlockSpec(memory_space=pltpu.VMEM),
        out_shape=jax.ShapeDtypeStruct((slots, 2, RB, width), jnp.bfloat16),
        scratch_shapes=[
            pltpu.VMEM((exposures, hin, window), jnp.bfloat16),
            pltpu.VMEM((exposures, hin, window), jnp.int32),
            pltpu.VMEM((2 * ph, window), jnp.bfloat16),
            pltpu.VMEM((exposures * blocks, 2, RB, width), jnp.bfloat16),
            pltpu.VMEM((per, kw, tw), jnp.bfloat16),
            pltpu.SemaphoreType.DMA((3, exposures)),
        ],
        compiler_params=pltpu.CompilerParams(vmem_limit_bytes=48 * 1024 * 1024),
        cost_estimate=pl.CostEstimate(
            flops=exposures * (8 * ph * hin * window + 4 * ph * kw * width),
            transcendentals=0,
            bytes_accessed=exposures * hin * window * 6 + per * kw * tw * 2 + slots * 2 * RB * width * 2,
        ),
    )(weights, send_idx, images, masks, row_kernels, col_kernel, previous)


def make_place_kernel(groups, capacity, positions, margin, inner):
    def kernel(rows_ref, *refs):
        recv_refs = refs[:groups]
        upper_ref, lower_ref, int_ref, canvas = refs[-4:]
        canvas[...] = jnp.zeros(canvas.shape, jnp.float32)
        for g in range(groups):
            def body(c, carry, g=g):
                pos = rows_ref[g * capacity + c]

                @pl.when((pos >= 0) & (pos < positions))
                def _():
                    canvas[pos] += recv_refs[g][c].astype(jnp.float32)

                return carry

            lax.fori_loop(0, capacity, body, 0)
        upper_ref[...] = canvas[0:margin].astype(jnp.bfloat16)
        lower_ref[...] = canvas[margin + inner :].astype(jnp.bfloat16)
        int_ref[...] = canvas[margin : margin + inner]

    return kernel


def place(rows, recvs, after, positions, margin, inner):
    after = list(after)
    groups = len(recvs)
    capacity = recvs[0].shape[0]
    block = recvs[0].shape[1:]
    return pl.pallas_call(
        make_place_kernel(groups, capacity, positions, margin, inner),
        in_specs=[pl.BlockSpec(memory_space=pltpu.SMEM)]
        + [pl.BlockSpec(memory_space=pltpu.VMEM)] * groups
        + [pl.BlockSpec(memory_space=pl.ANY)] * len(after),
        out_specs=[pl.BlockSpec(memory_space=pltpu.VMEM)] * 3,
        out_shape=[
            jax.ShapeDtypeStruct((margin,) + block, jnp.bfloat16),
            jax.ShapeDtypeStruct((margin,) + block, jnp.bfloat16),
            jax.ShapeDtypeStruct((inner,) + block, jnp.float32),
        ],
        scratch_shapes=[pltpu.VMEM((positions,) + block, jnp.float32)],
        compiler_params=pltpu.CompilerParams(vmem_limit_bytes=32 * 1024 * 1024),
    )(rows, *recvs, *after)


def local_body(images, masks, row_kernels, col_kernel, inv_var, dest_col, dest_row):
    exposures = images.shape[1]
    tile_width = col_kernel.shape[2]
    cw = col_kernel.shape[0] * tile_width
    pw = cw - 2 * tile_width
    tiles = col_kernel.shape[0]
    bounds = [tiles * sum(SPLIT[:i]) // sum(SPLIT) for i in range(len(SPLIT) + 1)]
    first_exp = lax.axis_index("skyx") * exposures
    weights = lax.dynamic_slice_in_dim(inv_var[0], first_exp, exposures)

    slot_dest = dest_col[0, :, 0]
    slot_rows = dest_row[0]
    slot_count = slot_dest.shape[0]
    peers = lax.axis_size("skyx")
    capacity = max(2, (3 * slot_count + 2 * peers - 1) // (2 * peers))
    positions = (PR + 2 * OVY) // RB
    offsets = (slot_dest - lax.axis_index("skyx")) % peers
    earlier = (jnp.arange(slot_count)[None, :] < jnp.arange(slot_count)[:, None]).astype(jnp.int32)
    onehot_dest = (offsets[:, None] == jnp.arange(peers)[None, :]).astype(jnp.int32)
    ranks = jnp.sum(jnp.dot(earlier, onehot_dest) * onehot_dest, axis=1)
    chosen = (offsets[None, None, :] == jnp.arange(peers)[:, None, None]) & (
        ranks[None, None, :] == jnp.arange(capacity)[None, :, None]
    )
    send_rows = jnp.sum(jnp.where(chosen, slot_rows[None, None, :] + 1, 0), axis=2) - 1
    send_idx = jnp.sum(jnp.where(chosen, jnp.arange(slot_count)[None, None, :] + 1, 0), axis=2) - 1
    send_idx = jnp.clip(send_idx, 0, slot_count - 1).reshape(-1)
    rings = [[(i, (i + step) % peers) for i in range(peers)] for step in range(peers)]
    table = lax.all_gather(jnp.stack([slot_dest, slot_rows]), "skyx")
    mine = (table[:, 0] == lax.axis_index("skyx")).astype(jnp.int32)
    mine_rank = jnp.dot(mine, earlier.T)
    picked = (mine[:, None, :] == 1) & (mine_rank[:, None, :] == jnp.arange(capacity)[None, :, None])
    recv_from = jnp.sum(jnp.where(picked, table[:, 1][:, None, :] + 1, 0), axis=2)
    sources = (lax.axis_index("skyx") - jnp.arange(peers)) % peers
    by_step = sources[:, None] == jnp.arange(peers)[None, :]
    recv_rows = jnp.sum(jnp.where(by_step[:, :, None], recv_from[None, :, :], 0), axis=1) - 1
    recv_rows = recv_rows.reshape(-1)

    margin = OVY // RB
    inner = PR // RB
    interiors = {}
    after = [recv_rows]
    previous = send_idx
    for chunk in ORDER:
        per = bounds[chunk + 1] - bounds[chunk]
        send_buf = warp_chunk(bounds[chunk], per, weights, send_idx, images, masks, row_kernels, col_kernel, previous)
        previous = send_buf
        send_buf = send_buf.reshape((peers, capacity) + send_buf.shape[1:])
        recvs = [send_buf[0]] + [lax.ppermute(send_buf[step], "skyx", rings[step]) for step in range(1, peers)]
        upper, lower, interior = place(recv_rows, recvs, after, positions, margin, inner)
        from_above = shifted(lower, "skyy", 1)
        from_below = shifted(upper, "skyy", -1)
        from_above = from_above.astype(jnp.float32)
        from_below = from_below.astype(jnp.float32)
        after = [upper]
        interior = interior.at[:margin].add(from_above)
        interior = interior.at[inner - margin :].add(from_below)
        interiors[chunk] = interior

    left_edge = interiors[0]
    right_edge = interiors[len(SPLIT) - 1]
    width = right_edge.shape[-1]
    from_left = shifted(right_edge[..., width - tile_width :].astype(jnp.bfloat16), "skyx", 1)
    from_right = shifted(left_edge[..., :tile_width].astype(jnp.bfloat16), "skyx", -1)
    from_left = from_left.astype(jnp.float32)
    from_right = from_right.astype(jnp.float32)
    first = left_edge[..., tile_width:]
    first = first.at[..., :tile_width].add(from_left)
    last = right_edge[..., : width - tile_width]
    last = last.at[..., width - 2 * tile_width :].add(from_right)
    middle = [interiors[c] for c in range(1, len(SPLIT) - 1)]
    core = jnp.concatenate([first] + middle + [last], axis=-1)
    num = core[:, 0].reshape(PR, pw)
    den = core[:, 1].reshape(PR, pw)
    return num / jnp.maximum(den, 1.0)


def solution(mesh):
    in_specs = (
        P(("tract", "skyy"), "skyx", None, None),
        P(("tract", "skyy"), "skyx", None, None),
        P(("tract", "skyy"), "skyx", None, None),
        P("tract", None, None),
        P(("tract", "skyy"), None),
        P(("tract", "skyy"), "skyx", None),
        P(("tract", "skyy"), "skyx"),
    )
    out_specs = P(("tract", "skyy"), "skyx")
    return jax.shard_map(local_body, mesh=mesh, in_specs=in_specs, out_specs=out_specs, check_vma=False)
```

```python
import jax
import jax.numpy as jnp
from jax import lax
from jax.experimental import pallas as pl
from jax.experimental.pallas import tpu as pltpu
from jax.sharding import PartitionSpec as P


OVY = 64
PR = 128
RB = 8
SPLIT = (5, 8, 6, 3, 2, 9)
ORDER = (0, 5, 1, 2, 3, 4)
ROW_PIECE = 640


def shifted(value, axis, steps):
    count = lax.axis_size(axis)
    first, last = (max(0, -steps), min(count, count - steps))
    return lax.ppermute(value, axis, [(source, source + steps) for source in range(first, last)])


def make_warp_kernel(start, width, first_tile, exposures, groups):
    def kernel(w_ref, idx_ref, img_hbm, mask_hbm, rk_ref, ck_hbm, prev_ref, *refs):
        out_refs = refs[:groups]
        img_buf, mask_buf, rw_buf, blk_buf, ck_ref, sems = refs[groups:]
        ph = rk_ref.shape[2]
        tiles, kw, tw = ck_ref.shape
        blocks = ph // RB
        ck_copy = pltpu.make_async_copy(ck_hbm.at[pl.ds(first_tile, tiles)], ck_ref, sems.at[2, 0])
        ck_copy.start()
        copies = []
        for e in range(exposures):
            ci = pltpu.make_async_copy(img_hbm.at[0, e, :, pl.ds(start, width)], img_buf.at[e], sems.at[0, e])
            cm = pltpu.make_async_copy(mask_hbm.at[0, e, :, pl.ds(start, width)], mask_buf.at[e], sems.at[1, e])
            ci.start()
            cm.start()
            copies.append((ci, cm))
        for e in range(exposures):
            ci, cm = copies[e]
            ci.wait()
            cm.wait()
            rk = rk_ref[0, e]
            if e == 0:
                ck_copy.wait()
            piece_start = 0
            while piece_start < width:
                piece = min(ROW_PIECE, width - piece_start)
                cols = pl.ds(piece_start, piece)
                good = mask_buf[e, :, cols] == 0
                img = img_buf[e, :, cols]
                p0 = jnp.where(good, img, jnp.zeros_like(img))
                p1 = good.astype(jnp.bfloat16)
                rw_buf[0:ph, cols] = jnp.dot(rk, p0, preferred_element_type=jnp.float32).astype(jnp.bfloat16)
                rw_buf[ph : 2 * ph, cols] = jnp.dot(rk, p1, preferred_element_type=jnp.float32).astype(jnp.bfloat16)
                piece_start += piece
            weight = w_ref[e]

            def tile(t, carry):
                off = pl.multiple_of(t * tw, tw)
                x = rw_buf[:, pl.ds(off, kw)]
                r = jnp.dot(x, ck_ref[t], preferred_element_type=jnp.float32) * weight
                rows = pl.ds(e * blocks, blocks)
                blk_buf[rows, 0, :, pl.ds(off, tw)] = r[0:ph].reshape(blocks, RB, tw).astype(jnp.bfloat16)
                blk_buf[rows, 1, :, pl.ds(off, tw)] = r[ph : 2 * ph].reshape(blocks, RB, tw).astype(jnp.bfloat16)
                return carry

            lax.fori_loop(0, tiles, tile, 0)

        capacity = out_refs[0].shape[0]
        for g in range(groups):
            def gather(slot, carry, g=g):
                out_refs[g][slot] = blk_buf[idx_ref[g * capacity + slot]]
                return carry

            lax.fori_loop(0, capacity, gather, 0)

    return kernel


def warp_chunk(first_tile, per, groups, weights, send_idx, images, masks, row_kernels, col_kernel, previous):
    _, exposures, hin, _ = images.shape
    ph = row_kernels.shape[2]
    _, kw, tw = col_kernel.shape
    width = per * tw
    window = width + kw - tw
    start = first_tile * tw
    blocks = ph // RB
    slots = send_idx.shape[0]
    return pl.pallas_call(
        make_warp_kernel(start, window, first_tile, exposures, groups),
        in_specs=[
            pl.BlockSpec(memory_space=pltpu.SMEM),
            pl.BlockSpec(memory_space=pltpu.SMEM),
            pl.BlockSpec(memory_space=pl.ANY),
            pl.BlockSpec(memory_space=pl.ANY),
            pl.BlockSpec(memory_space=pltpu.VMEM),
            pl.BlockSpec(memory_space=pl.ANY),
            pl.BlockSpec(memory_space=pl.ANY),
        ],
        out_specs=[pl.BlockSpec(memory_space=pltpu.VMEM)] * groups,
        out_shape=[jax.ShapeDtypeStruct((slots // groups, 2, RB, width), jnp.bfloat16)] * groups,
        scratch_shapes=[
            pltpu.VMEM((exposures, hin, window), jnp.bfloat16),
            pltpu.VMEM((exposures, hin, window), jnp.int32),
            pltpu.VMEM((2 * ph, window), jnp.bfloat16),
            pltpu.VMEM((exposures * blocks, 2, RB, width), jnp.bfloat16),
            pltpu.VMEM((per, kw, tw), jnp.bfloat16),
            pltpu.SemaphoreType.DMA((3, exposures)),
        ],
        compiler_params=pltpu.CompilerParams(vmem_limit_bytes=48 * 1024 * 1024),
        cost_estimate=pl.CostEstimate(
            flops=exposures * (8 * ph * hin * window + 4 * ph * kw * width),
            transcendentals=0,
            bytes_accessed=exposures * hin * window * 6 + per * kw * tw * 2 + slots * 2 * RB * width * 2,
        ),
    )(weights, send_idx, images, masks, row_kernels, col_kernel, previous)


def make_place_kernel(groups, capacity, positions, margin, inner):
    def kernel(rows_ref, *refs):
        recv_refs = refs[:groups]
        upper_ref, lower_ref, int_ref, canvas = refs[-4:]
        canvas[...] = jnp.zeros(canvas.shape, jnp.float32)
        for g in range(groups):
            def body(c, carry, g=g):
                pos = rows_ref[g * capacity + c]

                @pl.when((pos >= 0) & (pos < positions))
                def _():
                    canvas[pos] += recv_refs[g][c].astype(jnp.float32)

                return carry

            lax.fori_loop(0, capacity, body, 0)
        upper_ref[...] = canvas[0:margin].astype(jnp.bfloat16)
        lower_ref[...] = canvas[margin + inner :].astype(jnp.bfloat16)
        int_ref[...] = canvas[margin : margin + inner]

    return kernel


def place(rows, recvs, after, positions, margin, inner):
    after = list(after)
    groups = len(recvs)
    capacity = recvs[0].shape[0]
    block = recvs[0].shape[1:]
    return pl.pallas_call(
        make_place_kernel(groups, capacity, positions, margin, inner),
        in_specs=[pl.BlockSpec(memory_space=pltpu.SMEM)]
        + [pl.BlockSpec(memory_space=pltpu.VMEM)] * groups
        + [pl.BlockSpec(memory_space=pl.ANY)] * len(after),
        out_specs=[pl.BlockSpec(memory_space=pltpu.VMEM)] * 3,
        out_shape=[
            jax.ShapeDtypeStruct((margin,) + block, jnp.bfloat16),
            jax.ShapeDtypeStruct((margin,) + block, jnp.bfloat16),
            jax.ShapeDtypeStruct((inner,) + block, jnp.float32),
        ],
        scratch_shapes=[pltpu.VMEM((positions,) + block, jnp.float32)],
        compiler_params=pltpu.CompilerParams(vmem_limit_bytes=32 * 1024 * 1024),
    )(rows, *recvs, *after)


def local_body(images, masks, row_kernels, col_kernel, inv_var, dest_col, dest_row):
    exposures = images.shape[1]
    tile_width = col_kernel.shape[2]
    cw = col_kernel.shape[0] * tile_width
    pw = cw - 2 * tile_width
    tiles = col_kernel.shape[0]
    bounds = [tiles * sum(SPLIT[:i]) // sum(SPLIT) for i in range(len(SPLIT) + 1)]
    first_exp = lax.axis_index("skyx") * exposures
    weights = lax.dynamic_slice_in_dim(inv_var[0], first_exp, exposures)

    slot_dest = dest_col[0, :, 0]
    slot_rows = dest_row[0]
    slot_count = slot_dest.shape[0]
    peers = lax.axis_size("skyx")
    capacity = max(2, (3 * slot_count + 2 * peers - 1) // (2 * peers))
    positions = (PR + 2 * OVY) // RB
    offsets = (slot_dest - lax.axis_index("skyx")) % peers
    earlier = (jnp.arange(slot_count)[None, :] < jnp.arange(slot_count)[:, None]).astype(jnp.int32)
    onehot_dest = (offsets[:, None] == jnp.arange(peers)[None, :]).astype(jnp.int32)
    ranks = jnp.sum(jnp.dot(earlier, onehot_dest) * onehot_dest, axis=1)
    chosen = (offsets[None, None, :] == jnp.arange(peers)[:, None, None]) & (
        ranks[None, None, :] == jnp.arange(capacity)[None, :, None]
    )
    send_rows = jnp.sum(jnp.where(chosen, slot_rows[None, None, :] + 1, 0), axis=2) - 1
    send_idx = jnp.sum(jnp.where(chosen, jnp.arange(slot_count)[None, None, :] + 1, 0), axis=2) - 1
    send_idx = jnp.clip(send_idx, 0, slot_count - 1).reshape(-1)
    rings = [[(i, (i + step) % peers) for i in range(peers)] for step in range(peers)]
    recv_rows = [send_rows[0]] + [lax.ppermute(send_rows[step], "skyx", rings[step]) for step in range(1, peers)]
    recv_rows = jnp.concatenate(recv_rows)
    recv_rows = recv_rows.reshape(-1)

    margin = OVY // RB
    inner = PR // RB
    interiors = {}
    after = [recv_rows]
    previous = send_idx
    for chunk in ORDER:
        per = bounds[chunk + 1] - bounds[chunk]
        send_buf = warp_chunk(bounds[chunk], per, peers, weights, send_idx, images, masks, row_kernels, col_kernel, previous)
        previous = send_buf[-1]
        recvs = [send_buf[0]] + [lax.ppermute(send_buf[step], "skyx", rings[step]) for step in range(1, peers)]
        upper, lower, interior = place(recv_rows, recvs, after, positions, margin, inner)
        from_above = shifted(lower, "skyy", 1)
        from_below = shifted(upper, "skyy", -1)
        from_above = from_above.astype(jnp.float32)
        from_below = from_below.astype(jnp.float32)
        after = [upper]
        interior = interior.at[:margin].add(from_above)
        interior = interior.at[inner - margin :].add(from_below)
        interiors[chunk] = interior

    left_edge = interiors[0]
    right_edge = interiors[len(SPLIT) - 1]
    width = right_edge.shape[-1]
    from_left = shifted(right_edge[..., width - tile_width :].astype(jnp.bfloat16), "skyx", 1)
    from_right = shifted(left_edge[..., :tile_width].astype(jnp.bfloat16), "skyx", -1)
    from_left = from_left.astype(jnp.float32)
    from_right = from_right.astype(jnp.float32)
    first = left_edge[..., tile_width:]
    first = first.at[..., :tile_width].add(from_left)
    last = right_edge[..., : width - tile_width]
    last = last.at[..., width - 2 * tile_width :].add(from_right)
    middle = [interiors[c] for c in range(1, len(SPLIT) - 1)]
    core = jnp.concatenate([first] + middle + [last], axis=-1)
    num = core[:, 0].reshape(PR, pw)
    den = core[:, 1].reshape(PR, pw)
    return num / jnp.maximum(den, 1.0)


def solution(mesh):
    in_specs = (
        P(("tract", "skyy"), "skyx", None, None),
        P(("tract", "skyy"), "skyx", None, None),
        P(("tract", "skyy"), "skyx", None, None),
        P("tract", None, None),
        P(("tract", "skyy"), None),
        P(("tract", "skyy"), "skyx", None),
        P(("tract", "skyy"), "skyx"),
    )
    out_specs = P(("tract", "skyy"), "skyx")
    return jax.shard_map(local_body, mesh=mesh, in_specs=in_specs, out_specs=out_specs, check_vma=False)
```

```python
import jax
import jax.numpy as jnp
from jax import lax
from jax.experimental import pallas as pl
from jax.experimental.pallas import tpu as pltpu
from jax.sharding import PartitionSpec as P


OVY = 64
PR = 128
RB = 8
SPLIT = (5, 10, 9, 9)
ORDER = (0, 3, 1, 2)
ROW_PIECE = 640


def shifted(value, axis, steps):
    count = lax.axis_size(axis)
    first, last = (max(0, -steps), min(count, count - steps))
    return lax.ppermute(value, axis, [(source, source + steps) for source in range(first, last)])


def make_warp_kernel(start, width, first_tile, exposures, groups):
    def kernel(w_ref, idx_ref, img_hbm, mask_hbm, rk_ref, ck_hbm, prev_ref, *refs):
        out_refs = refs[:groups]
        img_buf, mask_buf, rw_buf, blk_buf, ck_ref, sems = refs[groups:]
        ph = rk_ref.shape[3]
        tiles, kw, tw = ck_ref.shape
        blocks = ph // RB
        ck_copy = pltpu.make_async_copy(ck_hbm.at[pl.ds(first_tile, tiles)], ck_ref, sems.at[2, 0])
        ck_copy.start()
        copies = []
        for e in range(exposures):
            ci = pltpu.make_async_copy(img_hbm.at[0, e, :, pl.ds(start, width)], img_buf.at[e], sems.at[0, e])
            cm = pltpu.make_async_copy(mask_hbm.at[0, e, :, pl.ds(start, width)], mask_buf.at[e], sems.at[1, e])
            ci.start()
            cm.start()
            copies.append((ci, cm))
        for e in range(exposures):
            ci, cm = copies[e]
            ci.wait()
            cm.wait()
            rk = rk_ref[0, e]
            if e == 0:
                ck_copy.wait()
            piece_start = 0
            while piece_start < width:
                piece = min(ROW_PIECE, width - piece_start)
                cols = pl.ds(piece_start, piece)
                good = mask_buf[e, :, cols] == 0
                img = img_buf[e, :, cols]
                p0 = jnp.where(good, img, jnp.zeros_like(img))
                p1 = good.astype(jnp.bfloat16)
                rw_buf[0:ph, cols] = lax.dot_general(
                    rk, p0, (((0,), (0,)), ((), ())), preferred_element_type=jnp.float32
                ).astype(jnp.bfloat16)
                rw_buf[ph : 2 * ph, cols] = lax.dot_general(
                    rk, p1, (((0,), (0,)), ((), ())), preferred_element_type=jnp.float32
                ).astype(jnp.bfloat16)
                piece_start += piece
            weight = w_ref[e]

            def tile(t, carry):
                off = pl.multiple_of(t * tw, tw)
                x = rw_buf[:, pl.ds(off, kw)]
                r = jnp.dot(x, ck_ref[t], preferred_element_type=jnp.float32) * weight
                rows = pl.ds(e * blocks, blocks)
                blk_buf[rows, 0, :, pl.ds(off, tw)] = r[0:ph].reshape(blocks, RB, tw).astype(jnp.bfloat16)
                blk_buf[rows, 1, :, pl.ds(off, tw)] = r[ph : 2 * ph].reshape(blocks, RB, tw).astype(jnp.bfloat16)
                return carry

            lax.fori_loop(0, tiles, tile, 0)

        capacity = out_refs[0].shape[0]
        for g in range(groups):
            def gather(slot, carry, g=g):
                out_refs[g][slot] = blk_buf[idx_ref[g * capacity + slot]]
                return carry

            lax.fori_loop(0, capacity, gather, 0)

    return kernel


def warp_chunk(first_tile, per, groups, weights, send_idx, images, masks, row_kernels, col_kernel, previous):
    _, exposures, hin, _ = images.shape
    ph = row_kernels.shape[2]
    _, kw, tw = col_kernel.shape
    width = per * tw
    window = width + kw - tw
    start = first_tile * tw
    blocks = ph // RB
    slots = send_idx.shape[0]
    return pl.pallas_call(
        make_warp_kernel(start, window, first_tile, exposures, groups),
        in_specs=[
            pl.BlockSpec(memory_space=pltpu.SMEM),
            pl.BlockSpec(memory_space=pltpu.SMEM),
            pl.BlockSpec(memory_space=pl.ANY),
            pl.BlockSpec(memory_space=pl.ANY),
            pl.BlockSpec(memory_space=pltpu.VMEM),
            pl.BlockSpec(memory_space=pl.ANY),
            pl.BlockSpec(memory_space=pl.ANY),
        ],
        out_specs=[pl.BlockSpec(memory_space=pltpu.VMEM)] * groups,
        out_shape=[jax.ShapeDtypeStruct((slots // groups, 2, RB, width), jnp.bfloat16)] * groups,
        scratch_shapes=[
            pltpu.VMEM((exposures, hin, window), jnp.bfloat16),
            pltpu.VMEM((exposures, hin, window), jnp.int32),
            pltpu.VMEM((2 * ph, window), jnp.bfloat16),
            pltpu.VMEM((exposures * blocks, 2, RB, width), jnp.bfloat16),
            pltpu.VMEM((per, kw, tw), jnp.bfloat16),
            pltpu.SemaphoreType.DMA((3, exposures)),
        ],
        compiler_params=pltpu.CompilerParams(vmem_limit_bytes=48 * 1024 * 1024),
        cost_estimate=pl.CostEstimate(
            flops=exposures * (8 * ph * hin * window + 4 * ph * kw * width),
            transcendentals=0,
            bytes_accessed=exposures * hin * window * 6 + per * kw * tw * 2 + slots * 2 * RB * width * 2,
        ),
    )(weights, send_idx, images, masks, jnp.swapaxes(row_kernels, 2, 3), col_kernel, previous)


def make_place_kernel(groups, capacity, positions, margin, inner):
    def kernel(rows_ref, *refs):
        recv_refs = refs[:groups]
        upper_ref, lower_ref, int_ref, canvas = refs[-4:]
        canvas[...] = jnp.zeros(canvas.shape, jnp.float32)
        for g in range(groups):
            def body(c, carry, g=g):
                pos = rows_ref[g * capacity + c]

                @pl.when((pos >= 0) & (pos < positions))
                def _():
                    canvas[pos] += recv_refs[g][c].astype(jnp.float32)

                return carry

            lax.fori_loop(0, capacity, body, 0)
        upper_ref[...] = canvas[0:margin].astype(jnp.bfloat16)
        lower_ref[...] = canvas[margin + inner :].astype(jnp.bfloat16)
        int_ref[...] = canvas[margin : margin + inner]

    return kernel


def place(rows, recvs, after, positions, margin, inner):
    after = list(after)
    groups = len(recvs)
    capacity = recvs[0].shape[0]
    block = recvs[0].shape[1:]
    return pl.pallas_call(
        make_place_kernel(groups, capacity, positions, margin, inner),
        in_specs=[pl.BlockSpec(memory_space=pltpu.SMEM)]
        + [pl.BlockSpec(memory_space=pltpu.VMEM)] * groups
        + [pl.BlockSpec(memory_space=pl.ANY)] * len(after),
        out_specs=[pl.BlockSpec(memory_space=pltpu.VMEM)] * 3,
        out_shape=[
            jax.ShapeDtypeStruct((margin,) + block, jnp.bfloat16),
            jax.ShapeDtypeStruct((margin,) + block, jnp.bfloat16),
            jax.ShapeDtypeStruct((inner,) + block, jnp.float32),
        ],
        scratch_shapes=[pltpu.VMEM((positions,) + block, jnp.float32)],
        compiler_params=pltpu.CompilerParams(vmem_limit_bytes=32 * 1024 * 1024),
    )(rows, *recvs, *after)


def local_body(images, masks, row_kernels, col_kernel, inv_var, dest_col, dest_row):
    exposures = images.shape[1]
    tile_width = col_kernel.shape[2]
    cw = col_kernel.shape[0] * tile_width
    pw = cw - 2 * tile_width
    tiles = col_kernel.shape[0]
    bounds = [tiles * sum(SPLIT[:i]) // sum(SPLIT) for i in range(len(SPLIT) + 1)]
    first_exp = lax.axis_index("skyx") * exposures
    weights = lax.dynamic_slice_in_dim(inv_var[0], first_exp, exposures)

    slot_dest = dest_col[0, :, 0]
    slot_rows = dest_row[0]
    slot_count = slot_dest.shape[0]
    peers = lax.axis_size("skyx")
    capacity = max(2, (3 * slot_count + 2 * peers - 1) // (2 * peers))
    positions = (PR + 2 * OVY) // RB
    offsets = (slot_dest - lax.axis_index("skyx")) % peers
    earlier = (jnp.arange(slot_count)[None, :] < jnp.arange(slot_count)[:, None]).astype(jnp.int32)
    onehot_dest = (offsets[:, None] == jnp.arange(peers)[None, :]).astype(jnp.int32)
    ranks = jnp.sum(jnp.dot(earlier, onehot_dest) * onehot_dest, axis=1)
    chosen = (offsets[None, None, :] == jnp.arange(peers)[:, None, None]) & (
        ranks[None, None, :] == jnp.arange(capacity)[None, :, None]
    )
    send_rows = jnp.sum(jnp.where(chosen, slot_rows[None, None, :] + 1, 0), axis=2) - 1
    send_idx = jnp.sum(jnp.where(chosen, jnp.arange(slot_count)[None, None, :] + 1, 0), axis=2) - 1
    send_idx = jnp.clip(send_idx, 0, slot_count - 1).reshape(-1)
    rings = [[(i, (i + step) % peers) for i in range(peers)] for step in range(peers)]
    recv_rows = [send_rows[0]] + [lax.ppermute(send_rows[step], "skyx", rings[step]) for step in range(1, peers)]
    recv_rows = jnp.concatenate(recv_rows)
    recv_rows = recv_rows.reshape(-1)

    margin = OVY // RB
    inner = PR // RB
    interiors = {}
    after = [recv_rows]
    previous = send_idx
    for chunk in ORDER:
        per = bounds[chunk + 1] - bounds[chunk]
        send_buf = warp_chunk(bounds[chunk], per, peers, weights, send_idx, images, masks, row_kernels, col_kernel, previous)
        previous = send_buf[-1]
        recvs = [send_buf[0]] + [lax.ppermute(send_buf[step], "skyx", rings[step]) for step in range(1, peers)]
        upper, lower, interior = place(recv_rows, recvs, after, positions, margin, inner)
        from_above = shifted(lower, "skyy", 1)
        from_below = shifted(upper, "skyy", -1)
        from_above = from_above.astype(jnp.float32)
        from_below = from_below.astype(jnp.float32)
        after = [upper]
        interior = interior.at[:margin].add(from_above)
        interior = interior.at[inner - margin :].add(from_below)
        interiors[chunk] = interior

    left_edge = interiors[0]
    right_edge = interiors[len(SPLIT) - 1]
    width = right_edge.shape[-1]
    from_left = shifted(right_edge[..., width - tile_width :].astype(jnp.bfloat16), "skyx", 1)
    from_right = shifted(left_edge[..., :tile_width].astype(jnp.bfloat16), "skyx", -1)
    from_left = from_left.astype(jnp.float32)
    from_right = from_right.astype(jnp.float32)
    first = left_edge[..., tile_width:]
    first = first.at[..., :tile_width].add(from_left)
    last = right_edge[..., : width - tile_width]
    last = last.at[..., width - 2 * tile_width :].add(from_right)
    middle = [interiors[c] for c in range(1, len(SPLIT) - 1)]
    core = jnp.concatenate([first] + middle + [last], axis=-1)
    num = core[:, 0].reshape(PR, pw)
    den = core[:, 1].reshape(PR, pw)
    return num / jnp.maximum(den, 1.0)


def solution(mesh):
    in_specs = (
        P(("tract", "skyy"), "skyx", None, None),
        P(("tract", "skyy"), "skyx", None, None),
        P(("tract", "skyy"), "skyx", None, None),
        P("tract", None, None),
        P(("tract", "skyy"), None),
        P(("tract", "skyy"), "skyx", None),
        P(("tract", "skyy"), "skyx"),
    )
    out_specs = P(("tract", "skyy"), "skyx")
    return jax.shard_map(local_body, mesh=mesh, in_specs=in_specs, out_specs=out_specs, check_vma=False)
```
